256 devices in a mesh: ctx: 32 (over y, z), tp: 8 (over x, core).
Axes of the slice: x: 4, y: 4, z: 8, core: 2. Of those that a mesh axis runs over, the one named last changes fastest.
Arguments:
- residual: bfloat16 [8192, 8192], P('ctx', 'tp'), may hold values from -90 to 90
- hyena_gate: bfloat16 [8192, 8192], P('ctx', 'tp'), may hold values from -6 to 6
- hyena_key: bfloat16 [8192, 8192], P('ctx', 'tp'), may hold values from -6 to 6
- hyena_value: bfloat16 [8192, 8192], P('ctx', 'tp'), may hold values from -6 to 6
- filter_taps: float32 [512, 128], P('tp'), may hold values from -0.45 to 0.45
- norm_gain: float32 [8192], P('tp'), may hold values from 0.5 to 1.5
- att_query: bfloat16 [8192, 8192], P('ctx', 'tp'), may hold values from -180 to 180
- att_key: bfloat16 [8192, 8192], P('ctx', 'tp'), may hold values from -6 to 6
- att_value: bfloat16 [8192, 8192], P('ctx', 'tp'), may hold values from -6 to 6
- doc_lengths: int32 [32], replicated, may hold values from 1 to 768, 8192 in all
Outputs:
- normed: bfloat16 [8192, 8192], P('ctx', 'tp')
- attended: bfloat16 [8192, 8192], P('ctx', 'tp')
The draws below stay inside these ranges and needn't reach their ends.
Inputs may be any that keep to these rules, and one draw needn't show every extreme that they name: `doc_lengths`: the lengths sum to 8192; the longest document has exactly 768 tokens.
All inputs are finite; a program needn't handle non-finite values.
Results may differ from the reference program's by a relative error of at most 0.0075.
Values may be sent and summed in bfloat16 or wider, within the bound.
No kernel may reach another device: no remote copies, remote signals or barrier semaphores. Data moves between devices by JAX's collectives and lax.ppermute only.
A program may use at most 128 MiB of HBM per device.

```python
import math
import jax
import jax.numpy as jnp
import numpy as np
from jax import lax

D = 8192
HEADS = 64
HEAD_DIM = 128
TAPS = 128
REACH = 3
TOK_DEV = 256
GROUPS = 512
SEQ = 8192
MAXDOC = 768
NDOCS = 32
N_CTX = 32


def draw_residual(key, part):
    base = jax.random.truncated_normal(key, -6.0, 6.0, (SEQ, D), jnp.float32)
    ramp = 0.5 * jnp.sqrt(1.0 + 8.0 * jnp.arange(D, dtype=jnp.float32) / (D - 1))
    values = base * ramp[None, :]
    return values.astype(jnp.bfloat16)


def attention_pair(key):
    base = jax.random.fold_in(key, 7)
    query_key, keys_key = jax.random.split(base)
    shape = (SEQ, HEADS * HEAD_DIM)
    query = jax.random.truncated_normal(query_key, -6.0, 6.0, shape, jnp.float32)
    keys = jax.random.truncated_normal(keys_key, -6.0, 6.0, shape, jnp.float32)
    return (query, keys)


def draw_att_query(key, part):
    return attention_pair(key)[0].astype(jnp.bfloat16)


def draw_att_key(key, part):
    return attention_pair(key)[1].astype(jnp.bfloat16)


def block_levels(key, shape, cuts, low, largest):
    def one(axis_at, shards_of):
        draws = jax.random.uniform(jax.random.fold_in(jax.random.fold_in(key, 6), axis_at), (shards_of,), jnp.float32, low / len(cuts), largest / len(cuts))
        return jnp.repeat(jnp.exp(draws), shape[axis_at] // shards_of).reshape((-1,) + (1,) * (len(shape) - axis_at - 1))

    level = one(*cuts[0])
    for cut in cuts[1:]:
        level = level * one(*cut)
    return level


def split_up(amount, total, limit, slope):
    weights = [(1 << 20) // math.isqrt(grade ** slope) + 1 for grade in range(2, amount + 1)]
    surplus, given = total - limit - (amount - 1), [1] * (amount - 1)
    while surplus > 0:
        movable = [i for i in range(amount - 1) if given[i] < limit]
        whole, remaining = sum([weights[i] for i in movable]), surplus
        for i in movable:
            more = min(limit - given[i], max(1, remaining * weights[i] // whole), surplus)
            given[i] = given[i] + more
            surplus = surplus - more
    return np.array([limit] + given)


def uneven_parts(stream_key, count, total, most, lean):
    if count == 2:
        one = jax.random.randint(stream_key, (), max(1, total - most), min(most, total - 1) + 1)
        return jnp.stack([one, total - one])
    sizes = jnp.asarray(split_up(count, total, most, lean), jnp.int32)
    twos = (count - 1) // 2
    donor, receiver = sizes[1:1 + 2 * twos:2], sizes[2:2 + 2 * twos:2]
    room = jnp.minimum(donor - 1, most - receiver)
    shifted = jax.random.randint(jax.random.fold_in(stream_key, 1), (twos,), 0, 1 << 20) % (room + 1)
    sizes = sizes.at[1:1 + 2 * twos:2].set(donor - shifted).at[2:2 + 2 * twos:2].set(receiver + shifted)
    return sizes[jax.random.permutation(jax.random.fold_in(stream_key, 2), count)]


def scatter_about(stream_key, dims, deviation, bound, cuts=(), held_as=jnp.bfloat16):
    entries = jax.random.normal(stream_key, dims, jnp.float32) * deviation
    if len(cuts) > 0:
        entries = block_levels(stream_key, dims, cuts, -0.22, 0.18) * entries
    return jnp.clip(entries, min=-bound, max=bound).astype(held_as)


def setup_inputs(seed: int = 0) -> dict:
    streams_of = jax.random.split(jax.random.key(seed), 11)
    residual = draw_residual(jax.random.fold_in(streams_of[10], 71), 0)
    hyena_gate = scatter_about(streams_of[1], (SEQ, D), 1.0, 6.0, ((0, 32), (1, 8)))
    hyena_key = scatter_about(streams_of[2], (SEQ, D), 1.0, 6.0, ((0, 32), (1, 8)))
    hyena_value = scatter_about(streams_of[3], (SEQ, D), 1.0, 6.0, ((0, 32), (1, 8)))
    filter_taps = scatter_about(streams_of[4], (GROUPS, TAPS), 0.09, 0.45, ((0, 8),), jnp.float32)
    norm_gain = jnp.clip(1.0 + 0.1 * jax.random.normal(streams_of[5], (D,), jnp.float32), 0.5, 1.5)
    att_query = draw_att_query(jax.random.fold_in(streams_of[10], 71), 0)
    att_key = draw_att_key(jax.random.fold_in(streams_of[10], 71), 0)
    att_value = scatter_about(streams_of[8], (SEQ, HEADS * HEAD_DIM), 1.0, 6.0, ((0, 32), (1, 8)))
    doc_lengths = uneven_parts(streams_of[9], NDOCS, SEQ, MAXDOC, 2).astype(jnp.int32)
    return {"residual": residual, "hyena_gate": hyena_gate, "hyena_key": hyena_key, "hyena_value": hyena_value, "filter_taps": filter_taps, "norm_gain": norm_gain, "att_query": att_query, "att_key": att_key, "att_value": att_value, "doc_lengths": doc_lengths}


norm_epsilon = 1e-05

def document_begin(doc_lengths, positions):
    starts = jnp.cumsum(doc_lengths).astype(jnp.int32) - doc_lengths
    return lax.optimization_barrier(jnp.max(jnp.where(starts[None, :] <= positions[:, None], starts[None, :], 0), axis=1)).astype(jnp.int32)

def causal_filter(extended, filter_taps, reach_back, out_rows):
    groups, taps = filter_taps.shape
    channels = extended.shape[1]
    width = channels // groups
    lag_table = jnp.arange(taps, dtype=jnp.int32)[:, None] + (taps - 1) - jnp.arange(2 * taps - 1, dtype=jnp.int32)[None, :]
    inside = (lag_table >= 0) & (lag_table < taps)
    clipped = jnp.clip(lag_table, 0, taps - 1)
    toeplitz = jnp.where(inside[None], filter_taps[:, clipped], jnp.float32(0.0))

    def one_block(block_index):
        first = (block_index * taps).astype(jnp.int32)
        sources = lax.dynamic_slice_in_dim(extended, first, 2 * taps - 1, 0).astype(jnp.float32)
        sources = sources.reshape(2 * taps - 1, groups, width)
        limits = lax.dynamic_slice_in_dim(reach_back, first, taps, 0)
        valid = lag_table <= limits[:, None]
        kernel = jnp.where(valid[None], toeplitz, jnp.float32(0.0))
        result = jnp.einsum('gts,sgc->tgc', kernel, sources, precision=lax.Precision.HIGHEST)
        return result.reshape(taps, channels)
    blocks = lax.map(one_block, jnp.arange(out_rows // taps, dtype=jnp.int32))
    return blocks.reshape(out_rows, channels)

def attend_one(query_head, key_head, value_head, visible, scale):
    scores = lax.dot_general(query_head, key_head, (((1,), (1,)), ((), ())), preferred_element_type=jnp.float32) * scale
    scores = jnp.where(visible, scores, jnp.float32(-1e+30))
    top = lax.optimization_barrier(jnp.max(scores, axis=1, keepdims=True))
    expo = jnp.where(visible, jnp.exp(scores - top), jnp.float32(0.0))
    denominator = lax.optimization_barrier(jnp.sum(expo, axis=1, keepdims=True))
    summed = jnp.dot(expo.astype(jnp.bfloat16), value_head, preferred_element_type=jnp.float32)
    return (summed / denominator).astype(jnp.bfloat16)

def reference(residual, hyena_gate, hyena_key, hyena_value, filter_taps, norm_gain, att_query, att_key, att_value, doc_lengths):
    positions = jnp.arange(SEQ, dtype=jnp.int32)
    doc_begin = document_begin(doc_lengths, positions)
    mixed = (hyena_key.astype(jnp.float32) * hyena_value.astype(jnp.float32)).astype(jnp.bfloat16)
    extended = jnp.concatenate([jnp.zeros((TAPS - 1, D), jnp.bfloat16), mixed], axis=0)
    filtered = causal_filter(extended, filter_taps, positions - doc_begin, SEQ)
    hidden = residual.astype(jnp.float32) + hyena_gate.astype(jnp.float32) * filtered
    mean_square = lax.optimization_barrier(jnp.mean(hidden * hidden, axis=1, keepdims=True))
    normed = (hidden * lax.rsqrt(mean_square + norm_epsilon) * norm_gain[None, :]).astype(jnp.bfloat16)
    window = (REACH + 1) * TOK_DEV
    front = jnp.zeros((REACH * TOK_DEV, HEADS * HEAD_DIM), jnp.bfloat16)
    padded_keys = jnp.concatenate([front, att_key], axis=0)
    padded_values = jnp.concatenate([front, att_value], axis=0)
    scale = jnp.float32(1.0 / HEAD_DIM ** 0.5)

    def one_shard(block_index):
        first = (block_index * TOK_DEV).astype(jnp.int32)
        query_rows = lax.dynamic_slice_in_dim(att_query, first, TOK_DEV, 0)
        key_rows = lax.dynamic_slice_in_dim(padded_keys, first, window, 0)
        value_rows = lax.dynamic_slice_in_dim(padded_values, first, window, 0)
        query_pos = first + jnp.arange(TOK_DEV, dtype=jnp.int32)
        key_pos = first - REACH * TOK_DEV + jnp.arange(window, dtype=jnp.int32)
        begin_rows = lax.dynamic_slice_in_dim(doc_begin, first, TOK_DEV, 0)
        visible = (key_pos[None, :] <= query_pos[:, None]) & (key_pos[None, :] >= begin_rows[:, None])
        query_heads = query_rows.reshape(TOK_DEV, HEADS, HEAD_DIM).transpose(1, 0, 2)
        key_heads = key_rows.reshape(window, HEADS, HEAD_DIM).transpose(1, 0, 2)
        value_heads = value_rows.reshape(window, HEADS, HEAD_DIM).transpose(1, 0, 2)
        outputs = lax.map(lambda trio: attend_one(trio[0], trio[1], trio[2], visible, scale), (query_heads, key_heads, value_heads))
        return outputs.transpose(1, 0, 2).reshape(TOK_DEV, HEADS * HEAD_DIM)
    attended = lax.map(one_shard, jnp.arange(N_CTX, dtype=jnp.int32)).reshape(SEQ, HEADS * HEAD_DIM)
    return (normed, attended)
```

```python
import jax
import jax.numpy as jnp
from jax import lax
from jax.sharding import PartitionSpec as P

D = 8192
HEAD_DIM = 128
REACH = 3


norm_epsilon = 1e-05


def shifted(value, axis, steps):
    count = lax.axis_size(axis)
    first, last = (max(0, -steps), min(count, count - steps))
    return lax.ppermute(value, axis, [(source, source + steps) for source in range(first, last)])


def document_begin(doc_lengths, positions):
    count = doc_lengths.shape[0]
    order = jnp.arange(count, dtype=jnp.int32)
    before = order[None, :] < order[:, None]
    starts = jnp.sum(jnp.where(before, doc_lengths[None, :], 0), axis=1)
    return jnp.max(jnp.where(starts[None, :] <= positions[:, None], starts[None, :], 0), axis=1)


def causal_filter(extended, filter_taps, reach_back, out_rows):
    groups, taps = filter_taps.shape
    channels = extended.shape[1]
    width = channels // groups
    lag_table = (
        jnp.arange(taps, dtype=jnp.int32)[:, None]
        + (taps - 1)
        - jnp.arange(2 * taps - 1, dtype=jnp.int32)[None, :]
    )
    reversed_taps = filter_taps[:, ::-1]
    period = jnp.concatenate([reversed_taps, jnp.zeros((groups, taps), jnp.float32)], axis=1)
    tiled = jnp.tile(period, (1, taps))
    toeplitz = tiled[:, : taps * (2 * taps - 1)].reshape(groups, taps, 2 * taps - 1)
    upper_part = toeplitz.astype(jnp.bfloat16)
    lower_part = (toeplitz - upper_part.astype(jnp.float32)).astype(jnp.bfloat16)
    zero_half = jnp.zeros((), jnp.bfloat16)
    numbers = (((0,), (2,)), ((1,), (0,)))
    results = []
    for block_index in range(out_rows // taps):
        first = block_index * taps
        sources = extended[first : first + 2 * taps - 1].reshape(2 * taps - 1, groups, width)
        limits = reach_back[first : first + taps]
        valid = (lag_table <= limits[:, None])[None]
        kernel_upper = jnp.where(valid, upper_part, zero_half)
        kernel_lower = jnp.where(valid, lower_part, zero_half)
        result = lax.dot_general(sources, kernel_upper, numbers, preferred_element_type=jnp.float32)
        result = result + lax.dot_general(
            sources, kernel_lower, numbers, preferred_element_type=jnp.float32
        )
        results.append(result.transpose(2, 0, 1).reshape(taps, channels))
    return jnp.concatenate(results, axis=0)


def attend_one(query_head, key_head, value_head, visible, scale):
    scores = (
        lax.dot_general(
            query_head, key_head, (((1,), (1,)), ((), ())), preferred_element_type=jnp.float32
        )
        * scale
    )
    scores = jnp.where(visible, scores, jnp.float32(-1e30))
    top = jnp.max(scores, axis=1, keepdims=True)
    expo = jnp.where(visible, jnp.exp(scores - top), jnp.float32(0.0))
    denominator = jnp.sum(expo, axis=1, keepdims=True)
    summed = jnp.dot(expo.astype(jnp.bfloat16), value_head, preferred_element_type=jnp.float32)
    return (summed / denominator).astype(jnp.bfloat16)


def on_device(
    residual,
    hyena_gate,
    hyena_key,
    hyena_value,
    filter_taps,
    norm_gain,
    att_query,
    att_key,
    att_value,
    doc_lengths,
):
    tok_rows = residual.shape[0]
    taps = filter_taps.shape[1]
    shard_index = lax.axis_index("ctx")
    anchor = shard_index * tok_rows
    positions = anchor + jnp.arange(tok_rows, dtype=jnp.int32)
    doc_begin = document_begin(doc_lengths, positions)
    mixed_rows = (hyena_key.astype(jnp.float32) * hyena_value.astype(jnp.float32)).astype(
        jnp.bfloat16
    )
    rim_rows = shifted(mixed_rows[tok_rows - (taps - 1) :], "ctx", 1)
    extended = jnp.concatenate([rim_rows, mixed_rows], axis=0)
    filtered = causal_filter(extended, filter_taps, positions - doc_begin, tok_rows)
    hidden = residual.astype(jnp.float32) + hyena_gate.astype(jnp.float32) * filtered
    local_sum = jnp.sum(hidden * hidden, axis=1)
    mean_square = lax.psum(local_sum, "tp") / D
    normed = (hidden * lax.rsqrt(mean_square + norm_epsilon)[:, None] * norm_gain[None, :]).astype(
        jnp.bfloat16
    )
    key_pair = jnp.stack([att_key, att_value])
    pieces = []
    relayed = key_pair
    for _ in range(REACH):
        relayed = shifted(relayed, "ctx", 1)
        pieces.insert(0, relayed)
    key_rows = jnp.concatenate([piece[0] for piece in pieces] + [att_key], axis=0)
    value_rows = jnp.concatenate([piece[1] for piece in pieces] + [att_value], axis=0)
    window = key_rows.shape[0]
    key_pos = anchor - REACH * tok_rows + jnp.arange(window, dtype=jnp.int32)
    visible = (key_pos[None, :] <= positions[:, None]) & (key_pos[None, :] >= doc_begin[:, None])
    scale = jnp.float32(1.0 / HEAD_DIM**0.5)
    head_count = att_query.shape[1] // HEAD_DIM
    outputs = []
    for head_index in range(head_count):
        lower = head_index * HEAD_DIM
        upper = lower + HEAD_DIM
        outputs.append(
            attend_one(
                att_query[:, lower:upper],
                key_rows[:, lower:upper],
                value_rows[:, lower:upper],
                visible,
                scale,
            )
        )
    attended = jnp.concatenate(outputs, axis=1)
    return (normed, attended)


def solution(mesh):
    placed = (
        P("ctx", "tp"),
        P("ctx", "tp"),
        P("ctx", "tp"),
        P("ctx", "tp"),
        P("tp", None),
        P("tp"),
        P("ctx", "tp"),
        P("ctx", "tp"),
        P("ctx", "tp"),
        P(),
    )
    return jax.shard_map(
        on_device,
        mesh=mesh,
        in_specs=placed,
        out_specs=(P("ctx", "tp"), P("ctx", "tp")),
        check_vma=False,
    )
```

```python
import jax
import jax.numpy as jnp
from jax import lax
from jax.sharding import PartitionSpec as P

D = 8192
HEAD_DIM = 128
REACH = 3


norm_epsilon = 1e-05


def shifted(value, axis, steps):
    count = lax.axis_size(axis)
    first, last = (max(0, -steps), min(count, count - steps))
    return lax.ppermute(value, axis, [(source, source + steps) for source in range(first, last)])


def document_begin(doc_lengths, positions):
    count = doc_lengths.shape[0]
    order = jnp.arange(count, dtype=jnp.int32)
    before = order[None, :] < order[:, None]
    starts = jnp.sum(jnp.where(before, doc_lengths[None, :], 0), axis=1)
    return jnp.max(jnp.where(starts[None, :] <= positions[:, None], starts[None, :], 0), axis=1)


def causal_filter(extended, filter_taps, reach_back, out_rows):
    groups, taps = filter_taps.shape
    channels = extended.shape[1]
    width = channels // groups
    lag_table = (
        jnp.arange(taps, dtype=jnp.int32)[:, None]
        + (taps - 1)
        - jnp.arange(2 * taps - 1, dtype=jnp.int32)[None, :]
    )
    reversed_taps = filter_taps[:, ::-1]
    period = jnp.concatenate([reversed_taps, jnp.zeros((groups, taps), jnp.float32)], axis=1)
    tiled = jnp.tile(period, (1, taps))
    toeplitz = tiled[:, : taps * (2 * taps - 1)].reshape(groups, taps, 2 * taps - 1)
    upper_part = toeplitz.astype(jnp.bfloat16)
    lower_part = (toeplitz - upper_part.astype(jnp.float32)).astype(jnp.bfloat16)
    zero_half = jnp.zeros((), jnp.bfloat16)
    numbers = (((0,), (2,)), ((1,), (0,)))
    results = []
    for block_index in range(out_rows // taps):
        first = block_index * taps
        sources = extended[first : first + 2 * taps - 1].reshape(2 * taps - 1, groups, width)
        limits = reach_back[first : first + taps]
        valid = (lag_table <= limits[:, None])[None]
        kernel_upper = jnp.where(valid, upper_part, zero_half)
        kernel_lower = jnp.where(valid, lower_part, zero_half)
        result = lax.dot_general(sources, kernel_upper, numbers, preferred_element_type=jnp.float32)
        result = result + lax.dot_general(
            sources, kernel_lower, numbers, preferred_element_type=jnp.float32
        )
        results.append(result.transpose(2, 0, 1).reshape(taps, channels))
    return jnp.concatenate(results, axis=0)


def attend_part(query_head, key_head, value_head, visible, scale):
    scores = (
        lax.dot_general(
            query_head, key_head, (((1,), (1,)), ((), ())), preferred_element_type=jnp.float32
        )
        * scale
    )
    scores = jnp.where(visible, scores, jnp.float32(-1e30))
    top = jnp.max(scores, axis=1, keepdims=True)
    expo = jnp.where(visible, jnp.exp(scores - top), jnp.float32(0.0))
    denominator = jnp.sum(expo, axis=1, keepdims=True)
    summed = jnp.dot(expo.astype(jnp.bfloat16), value_head, preferred_element_type=jnp.float32)
    return summed, top, denominator


def attend_block(queries, keys, values, visible, scale):
    head_count = queries.shape[1] // HEAD_DIM
    sums, tops, dens = [], [], []
    for head_index in range(head_count):
        lower = head_index * HEAD_DIM
        upper = lower + HEAD_DIM
        summed, top, den = attend_part(
            queries[:, lower:upper], keys[:, lower:upper], values[:, lower:upper], visible, scale
        )
        sums.append(summed)
        tops.append(top)
        dens.append(den)
    return jnp.stack(sums, axis=1), jnp.concatenate(tops, axis=1), jnp.concatenate(dens, axis=1)


def on_device(
    residual,
    hyena_gate,
    hyena_key,
    hyena_value,
    filter_taps,
    norm_gain,
    att_query,
    att_key,
    att_value,
    doc_lengths,
):
    tok_rows = residual.shape[0]
    taps = filter_taps.shape[1]
    shard_index = lax.axis_index("ctx")
    anchor = shard_index * tok_rows
    positions = anchor + jnp.arange(tok_rows, dtype=jnp.int32)
    doc_begin = document_begin(doc_lengths, positions)
    mixed_rows = (hyena_key.astype(jnp.float32) * hyena_value.astype(jnp.float32)).astype(
        jnp.bfloat16
    )
    rim_rows = shifted(mixed_rows[tok_rows - (taps - 1) :], "ctx", 1)
    key_pair = jnp.stack([att_key, att_value])
    previous = shifted(key_pair, "ctx", 1)
    later_query = shifted(att_query, "ctx", -2)
    key_rows = jnp.concatenate([previous[0], att_key], axis=0)
    value_rows = jnp.concatenate([previous[1], att_value], axis=0)
    window = key_rows.shape[0]
    key_pos = anchor - tok_rows + jnp.arange(window, dtype=jnp.int32)
    scale = jnp.float32(1.0 / HEAD_DIM**0.5)
    far_pos = positions + 2 * tok_rows
    far_begin = document_begin(doc_lengths, far_pos)
    far_visible = (key_pos[None, :] <= far_pos[:, None]) & (key_pos[None, :] >= far_begin[:, None])
    far_sum, far_top, far_den = attend_block(later_query, key_rows, value_rows, far_visible, scale)
    far_packet = (far_sum.astype(jnp.bfloat16), far_top, far_den)
    far_packet, mixed_rows = lax.optimization_barrier((far_packet, mixed_rows))
    far_sum, far_top, far_den = shifted(far_packet, "ctx", 2)
    extended = jnp.concatenate([rim_rows, mixed_rows], axis=0)
    filtered = causal_filter(extended, filter_taps, positions - doc_begin, tok_rows)
    hidden = residual.astype(jnp.float32) + hyena_gate.astype(jnp.float32) * filtered
    local_sum = jnp.sum(hidden * hidden, axis=1)
    mean_square = lax.psum(local_sum, "tp") / D
    normed = (hidden * lax.rsqrt(mean_square + norm_epsilon)[:, None] * norm_gain[None, :]).astype(
        jnp.bfloat16
    )
    visible = (key_pos[None, :] <= positions[:, None]) & (key_pos[None, :] >= doc_begin[:, None])
    near_sum, near_top, near_den = attend_block(att_query, key_rows, value_rows, visible, scale)
    far_top = jnp.where(far_den > 0, far_top, jnp.float32(-1e30))
    top = jnp.maximum(near_top, far_top)
    near_scale = jnp.exp(near_top - top)
    far_scale = jnp.exp(far_top - top)
    denominator = near_den * near_scale + far_den * far_scale
    summed = near_sum * near_scale[:, :, None] + far_sum.astype(jnp.float32) * far_scale[:, :, None]
    attended = (summed / denominator[:, :, None]).astype(jnp.bfloat16).reshape(tok_rows, -1)
    return (normed, attended)


def solution(mesh):
    placed = (
        P("ctx", "tp"),
        P("ctx", "tp"),
        P("ctx", "tp"),
        P("ctx", "tp"),
        P("tp", None),
        P("tp"),
        P("ctx", "tp"),
        P("ctx", "tp"),
        P("ctx", "tp"),
        P(),
    )
    return jax.shard_map(
        on_device,
        mesh=mesh,
        in_specs=placed,
        out_specs=(P("ctx", "tp"), P("ctx", "tp")),
        check_vma=False,
    )
```

```python
import jax
import jax.numpy as jnp
from jax import lax
from jax.experimental import pallas as pl
from jax.experimental.pallas import tpu as pltpu
from jax.sharding import PartitionSpec as P

D = 8192
HEAD_DIM = 128
REACH = 3


norm_epsilon = 1e-05


def shifted(value, axis, steps):
    count = lax.axis_size(axis)
    first, last = (max(0, -steps), min(count, count - steps))
    return lax.ppermute(value, axis, [(source, source + steps) for source in range(first, last)])


def document_begin(doc_lengths, positions):
    count = doc_lengths.shape[0]
    order = jnp.arange(count, dtype=jnp.int32)
    before = order[None, :] < order[:, None]
    starts = jnp.sum(jnp.where(before, doc_lengths[None, :], 0), axis=1)
    return jnp.max(jnp.where(starts[None, :] <= positions[:, None], starts[None, :], 0), axis=1)


def toeplitz_rows(reversed_ref, out_ref):
    rows = out_ref.shape[1]
    for group in range(out_ref.shape[0]):
        line = jnp.broadcast_to(reversed_ref[group : group + 1, :], (rows, reversed_ref.shape[1]))
        out_ref[group] = pltpu.roll(line, 0, 1, stride=1, stride_axis=0)


def build_toeplitz(filter_taps):
    groups, taps = filter_taps.shape
    span = 2 * taps
    reversed_taps = jnp.concatenate(
        [filter_taps[:, ::-1], jnp.zeros((groups, span - taps), jnp.float32)], axis=1
    )
    step = 8
    return pl.pallas_call(
        toeplitz_rows,
        grid=(groups // step,),
        in_specs=[pl.BlockSpec((step, span), lambda i: (i, 0))],
        out_specs=pl.BlockSpec((step, taps, span), lambda i: (i, 0, 0)),
        out_shape=jax.ShapeDtypeStruct((groups, taps, span), jnp.float32),
    )(reversed_taps)


def causal_filter(extended, filter_taps, reach_back, out_rows):
    groups, taps = filter_taps.shape
    channels = extended.shape[1]
    width = channels // groups
    span = 2 * taps
    lag_table = (
        jnp.arange(taps, dtype=jnp.int32)[:, None]
        + (taps - 1)
        - jnp.arange(span, dtype=jnp.int32)[None, :]
    )
    toeplitz = build_toeplitz(filter_taps)
    upper_part = toeplitz.astype(jnp.bfloat16)
    lower_part = (toeplitz - upper_part.astype(jnp.float32)).astype(jnp.bfloat16)
    zero_half = jnp.zeros((), jnp.bfloat16)
    numbers = (((0,), (2,)), ((1,), (0,)))
    extended = jnp.concatenate([extended, jnp.zeros((1, channels), extended.dtype)], axis=0)
    results = []
    for block_index in range(out_rows // taps):
        first = block_index * taps
        sources = extended[first : first + span].reshape(span, groups, width)
        limits = reach_back[first : first + taps]
        valid = (lag_table <= limits[:, None])[None]
        kernel_upper = jnp.where(valid, upper_part, zero_half)
        kernel_lower = jnp.where(valid, lower_part, zero_half)
        result = lax.dot_general(sources, kernel_upper, numbers, preferred_element_type=jnp.float32)
        result = result + lax.dot_general(
            sources, kernel_lower, numbers, preferred_element_type=jnp.float32
        )
        results.append(result.transpose(2, 0, 1).reshape(taps, channels))
    return jnp.concatenate(results, axis=0)


def tp_sum(value):
    count = lax.axis_size("tp")
    stride = 1
    while stride < count:
        value = value + lax.ppermute(value, "tp", [(i, i ^ stride) for i in range(count)])
        stride *= 2
    return value


def attend_part(query_head, key_head, value_head, visible, scale):
    scores = (
        lax.dot_general(
            query_head, key_head, (((1,), (1,)), ((), ())), preferred_element_type=jnp.float32
        )
        * scale
    )
    scores = jnp.where(visible, scores, jnp.float32(-1e30))
    top = jnp.max(scores, axis=1, keepdims=True)
    expo = jnp.where(visible, jnp.exp(scores - top), jnp.float32(0.0))
    denominator = jnp.sum(expo, axis=1, keepdims=True)
    summed = jnp.dot(expo.astype(jnp.bfloat16), value_head, preferred_element_type=jnp.float32)
    return summed, top, denominator


def attend_block(queries, keys, values, visible, scale):
    head_count = queries.shape[1] // HEAD_DIM
    sums, tops, dens = [], [], []
    for head_index in range(head_count):
        lower = head_index * HEAD_DIM
        upper = lower + HEAD_DIM
        summed, top, den = attend_part(
            queries[:, lower:upper], keys[:, lower:upper], values[:, lower:upper], visible, scale
        )
        sums.append(summed)
        tops.append(top)
        dens.append(den)
    return jnp.stack(sums, axis=1), jnp.concatenate(tops, axis=1), jnp.concatenate(dens, axis=1)


def on_device(
    residual,
    hyena_gate,
    hyena_key,
    hyena_value,
    filter_taps,
    norm_gain,
    att_query,
    att_key,
    att_value,
    doc_lengths,
):
    tok_rows = residual.shape[0]
    taps = filter_taps.shape[1]
    shard_index = lax.axis_index("ctx")
    anchor = shard_index * tok_rows
    positions = anchor + jnp.arange(tok_rows, dtype=jnp.int32)
    doc_begin = document_begin(doc_lengths, positions)
    mixed_rows = (hyena_key.astype(jnp.float32) * hyena_value.astype(jnp.float32)).astype(
        jnp.bfloat16
    )
    rim_rows = shifted(mixed_rows[tok_rows - (taps - 1) :], "ctx", 1)
    key_pair = jnp.stack([att_key, att_value])
    previous = shifted(key_pair, "ctx", 1)
    later_query = shifted(att_query, "ctx", -2)
    key_rows = jnp.concatenate([previous[0], att_key], axis=0)
    value_rows = jnp.concatenate([previous[1], att_value], axis=0)
    window = key_rows.shape[0]
    key_pos = anchor - tok_rows + jnp.arange(window, dtype=jnp.int32)
    scale = jnp.float32(1.0 / HEAD_DIM**0.5)
    extended = jnp.concatenate([rim_rows, mixed_rows], axis=0)
    filtered = causal_filter(extended, filter_taps, positions - doc_begin, tok_rows)
    hidden = residual.astype(jnp.float32) + hyena_gate.astype(jnp.float32) * filtered
    local_sum = jnp.sum(hidden * hidden, axis=1)
    local_sum, later_query = lax.optimization_barrier((local_sum, later_query))
    mean_square = tp_sum(local_sum) / D
    normed = (hidden * lax.rsqrt(mean_square + norm_epsilon)[:, None] * norm_gain[None, :]).astype(
        jnp.bfloat16
    )
    far_pos = positions + 2 * tok_rows
    far_begin = document_begin(doc_lengths, far_pos)
    far_visible = (key_pos[None, :] <= far_pos[:, None]) & (key_pos[None, :] >= far_begin[:, None])
    far_sum, far_top, far_den = attend_block(later_query, key_rows, value_rows, far_visible, scale)
    far_stats = jnp.concatenate([far_top, far_den], axis=1)
    far_sum, far_stats = shifted((far_sum.astype(jnp.bfloat16), far_stats), "ctx", 2)
    head_count = far_top.shape[1]
    far_top, far_den = far_stats[:, :head_count], far_stats[:, head_count:]
    visible = (key_pos[None, :] <= positions[:, None]) & (key_pos[None, :] >= doc_begin[:, None])
    near_sum, near_top, near_den = attend_block(att_query, key_rows, value_rows, visible, scale)
    far_top = jnp.where(far_den > 0, far_top, jnp.float32(-1e30))
    top = jnp.maximum(near_top, far_top)
    near_scale = jnp.exp(near_top - top)
    far_scale = jnp.exp(far_top - top)
    denominator = near_den * near_scale + far_den * far_scale
    summed = near_sum * near_scale[:, :, None] + far_sum.astype(jnp.float32) * far_scale[:, :, None]
    attended = (summed / denominator[:, :, None]).astype(jnp.bfloat16).reshape(tok_rows, -1)
    return (normed, attended)


def solution(mesh):
    placed = (
        P("ctx", "tp"),
        P("ctx", "tp"),
        P("ctx", "tp"),
        P("ctx", "tp"),
        P("tp", None),
        P("tp"),
        P("ctx", "tp"),
        P("ctx", "tp"),
        P("ctx", "tp"),
        P(),
    )
    return jax.shard_map(
        on_device,
        mesh=mesh,
        in_specs=placed,
        out_specs=(P("ctx", "tp"), P("ctx", "tp")),
        check_vma=False,
    )
```

```python
import jax
import jax.numpy as jnp
from jax import lax
from jax.experimental import pallas as pl
from jax.experimental.pallas import tpu as pltpu
from jax.sharding import PartitionSpec as P

D = 8192
HEAD_DIM = 128
REACH = 3


norm_epsilon = 1e-05


def shifted(value, axis, steps):
    count = lax.axis_size(axis)
    first, last = (max(0, -steps), min(count, count - steps))
    return lax.ppermute(value, axis, [(source, source + steps) for source in range(first, last)])


def document_begin(doc_lengths, positions):
    count = doc_lengths.shape[0]
    order = jnp.arange(count, dtype=jnp.int32)
    before = order[None, :] < order[:, None]
    starts = jnp.sum(jnp.where(before, doc_lengths[None, :], 0), axis=1)
    return jnp.max(jnp.where(starts[None, :] <= positions[:, None], starts[None, :], 0), axis=1)


def toeplitz_rows(reversed_ref, out_ref):
    rows = out_ref.shape[1]
    for group in range(out_ref.shape[0]):
        line = jnp.broadcast_to(reversed_ref[group : group + 1, :], (rows, reversed_ref.shape[1]))
        out_ref[group] = pltpu.roll(line, 0, 1, stride=1, stride_axis=0)


def build_toeplitz(filter_taps):
    groups, taps = filter_taps.shape
    span = 2 * taps
    reversed_taps = jnp.concatenate(
        [filter_taps[:, ::-1], jnp.zeros((groups, span - taps), jnp.float32)], axis=1
    )
    step = 8
    return pl.pallas_call(
        toeplitz_rows,
        grid=(groups // step,),
        in_specs=[pl.BlockSpec((step, span), lambda i: (i, 0))],
        out_specs=pl.BlockSpec((step, taps, span), lambda i: (i, 0, 0)),
        out_shape=jax.ShapeDtypeStruct((groups, taps, span), jnp.float32),
    )(reversed_taps)


def causal_filter(extended, filter_taps, reach_back, out_rows):
    groups, taps = filter_taps.shape
    channels = extended.shape[1]
    width = channels // groups
    span = 2 * taps
    lag_table = (
        jnp.arange(taps, dtype=jnp.int32)[:, None]
        + (taps - 1)
        - jnp.arange(span, dtype=jnp.int32)[None, :]
    )
    toeplitz = build_toeplitz(filter_taps)
    upper_part = toeplitz.astype(jnp.bfloat16)
    lower_part = (toeplitz - upper_part.astype(jnp.float32)).astype(jnp.bfloat16)
    zero_half = jnp.zeros((), jnp.bfloat16)
    numbers = (((0,), (2,)), ((1,), (0,)))
    extended = jnp.concatenate([extended, jnp.zeros((1, channels), extended.dtype)], axis=0)
    results = []
    for block_index in range(out_rows // taps):
        first = block_index * taps
        sources = extended[first : first + span].reshape(span, groups, width)
        limits = reach_back[first : first + taps]
        valid = (lag_table <= limits[:, None])[None]
        kernel_upper = jnp.where(valid, upper_part, zero_half)
        kernel_lower = jnp.where(valid, lower_part, zero_half)
        result = lax.dot_general(sources, kernel_upper, numbers, preferred_element_type=jnp.float32)
        result = result + lax.dot_general(
            sources, kernel_lower, numbers, preferred_element_type=jnp.float32
        )
        results.append(result.transpose(2, 0, 1).reshape(taps, channels))
    return jnp.concatenate(results, axis=0)


def tp_sum(value):
    count = lax.axis_size("tp")
    stride = 1
    while stride < count:
        value = value + lax.ppermute(value, "tp", [(i, i ^ stride) for i in range(count)])
        stride *= 2
    return value


def attend_block(queries, keys, values, visible, scale):
    head_count = queries.shape[1] // HEAD_DIM
    query_heads = queries.reshape(queries.shape[0], head_count, HEAD_DIM)
    key_heads = keys.reshape(keys.shape[0], head_count, HEAD_DIM)
    value_heads = values.reshape(values.shape[0], head_count, HEAD_DIM)
    scores = (
        jnp.einsum("qhd,khd->hqk", query_heads, key_heads, preferred_element_type=jnp.float32)
        * scale
    )
    scores = jnp.where(visible[None], scores, jnp.float32(-1e30))
    top = jnp.max(scores, axis=2, keepdims=True)
    expo = jnp.where(visible[None], jnp.exp(scores - top), jnp.float32(0.0))
    denominator = jnp.sum(expo, axis=2)
    summed = jnp.einsum(
        "hqk,khd->qhd", expo.astype(jnp.bfloat16), value_heads, preferred_element_type=jnp.float32
    )
    return summed, top[:, :, 0].T, denominator.T


def on_device(
    residual,
    hyena_gate,
    hyena_key,
    hyena_value,
    filter_taps,
    norm_gain,
    att_query,
    att_key,
    att_value,
    doc_lengths,
):
    tok_rows = residual.shape[0]
    taps = filter_taps.shape[1]
    shard_index = lax.axis_index("ctx")
    anchor = shard_index * tok_rows
    positions = anchor + jnp.arange(tok_rows, dtype=jnp.int32)
    doc_begin = document_begin(doc_lengths, positions)
    mixed_rows = (hyena_key.astype(jnp.float32) * hyena_value.astype(jnp.float32)).astype(
        jnp.bfloat16
    )
    rim_rows = shifted(mixed_rows[tok_rows - (taps - 1) :], "ctx", 1)
    key_pair = jnp.stack([att_key, att_value])
    previous = shifted(key_pair, "ctx", 1)
    later_query = shifted(att_query, "ctx", -2)
    key_rows = jnp.concatenate([previous[0], att_key], axis=0)
    value_rows = jnp.concatenate([previous[1], att_value], axis=0)
    window = key_rows.shape[0]
    key_pos = anchor - tok_rows + jnp.arange(window, dtype=jnp.int32)
    scale = jnp.float32(1.0 / HEAD_DIM**0.5)
    extended = jnp.concatenate([rim_rows, mixed_rows], axis=0)
    filtered = causal_filter(extended, filter_taps, positions - doc_begin, tok_rows)
    hidden = residual.astype(jnp.float32) + hyena_gate.astype(jnp.float32) * filtered
    local_sum = jnp.sum(hidden * hidden, axis=1)
    local_sum, later_query = lax.optimization_barrier((local_sum, later_query))
    far_pos = positions + 2 * tok_rows
    far_begin = document_begin(doc_lengths, far_pos)
    far_visible = (key_pos[None, :] <= far_pos[:, None]) & (key_pos[None, :] >= far_begin[:, None])
    far_sum, far_top, far_den = attend_block(later_query, key_rows, value_rows, far_visible, scale)
    far_stats = jnp.concatenate([far_top, far_den], axis=1)
    far_packet = (far_sum.astype(jnp.bfloat16), far_stats)
    far_packet, local_sum, near_query = lax.optimization_barrier((far_packet, local_sum, att_query))
    far_sum, far_stats = shifted(far_packet, "ctx", 2)
    mean_square = tp_sum(local_sum) / D
    normed = (hidden * lax.rsqrt(mean_square + norm_epsilon)[:, None] * norm_gain[None, :]).astype(
        jnp.bfloat16
    )
    head_count = far_top.shape[1]
    far_top, far_den = far_stats[:, :head_count], far_stats[:, head_count:]
    visible = (key_pos[None, :] <= positions[:, None]) & (key_pos[None, :] >= doc_begin[:, None])
    near_sum, near_top, near_den = attend_block(near_query, key_rows, value_rows, visible, scale)
    far_top = jnp.where(far_den > 0, far_top, jnp.float32(-1e30))
    top = jnp.maximum(near_top, far_top)
    near_scale = jnp.exp(near_top - top)
    far_scale = jnp.exp(far_top - top)
    denominator = near_den * near_scale + far_den * far_scale
    summed = near_sum * near_scale[:, :, None] + far_sum.astype(jnp.float32) * far_scale[:, :, None]
    attended = (summed / denominator[:, :, None]).astype(jnp.bfloat16).reshape(tok_rows, -1)
    return (normed, attended)


def solution(mesh):
    placed = (
        P("ctx", "tp"),
        P("ctx", "tp"),
        P("ctx", "tp"),
        P("ctx", "tp"),
        P("tp", None),
        P("tp"),
        P("ctx", "tp"),
        P("ctx", "tp"),
        P("ctx", "tp"),
        P(),
    )
    return jax.shard_map(
        on_device,
        mesh=mesh,
        in_specs=placed,
        out_specs=(P("ctx", "tp"), P("ctx", "tp")),
        check_vma=False,
    )
```

```python
import jax
import jax.numpy as jnp
from jax import lax
from jax.experimental import pallas as pl
from jax.experimental.pallas import tpu as pltpu
from jax.sharding import PartitionSpec as P

D = 8192
HEAD_DIM = 128
REACH = 3


norm_epsilon = 1e-05


def shifted(value, axis, steps):
    count = lax.axis_size(axis)
    first, last = (max(0, -steps), min(count, count - steps))
    return lax.ppermute(value, axis, [(source, source + steps) for source in range(first, last)])


def document_begin(doc_lengths, positions):
    count = doc_lengths.shape[0]
    order = jnp.arange(count, dtype=jnp.int32)
    before = order[None, :] < order[:, None]
    starts = jnp.sum(jnp.where(before, doc_lengths[None, :], 0), axis=1)
    return jnp.max(jnp.where(starts[None, :] <= positions[:, None], starts[None, :], 0), axis=1)


def toeplitz_rows(reversed_ref, out_ref):
    rows = out_ref.shape[1]
    for group in range(out_ref.shape[0]):
        line = jnp.broadcast_to(reversed_ref[group : group + 1, :], (rows, reversed_ref.shape[1]))
        out_ref[group] = pltpu.roll(line, 0, 1, stride=1, stride_axis=0)


def build_toeplitz(filter_taps):
    groups, taps = filter_taps.shape
    span = 2 * taps
    reversed_taps = jnp.concatenate(
        [filter_taps[:, ::-1], jnp.zeros((groups, span - taps), jnp.float32)], axis=1
    )
    step = 8
    return pl.pallas_call(
        toeplitz_rows,
        grid=(groups // step,),
        in_specs=[pl.BlockSpec((step, span), lambda i: (i, 0))],
        out_specs=pl.BlockSpec((step, taps, span), lambda i: (i, 0, 0)),
        out_shape=jax.ShapeDtypeStruct((groups, taps, span), jnp.float32),
    )(reversed_taps)


def causal_filter(extended, filter_taps, reach_back, out_rows):
    groups, taps = filter_taps.shape
    channels = extended.shape[1]
    width = channels // groups
    span = 2 * taps
    lag_table = (
        jnp.arange(taps, dtype=jnp.int32)[:, None]
        + (taps - 1)
        - jnp.arange(span, dtype=jnp.int32)[None, :]
    )
    toeplitz = build_toeplitz(filter_taps)
    upper_part = toeplitz.astype(jnp.bfloat16)
    lower_part = (toeplitz - upper_part.astype(jnp.float32)).astype(jnp.bfloat16)
    zero_half = jnp.zeros((), jnp.bfloat16)
    numbers = (((0,), (2,)), ((1,), (0,)))
    extended = jnp.concatenate([extended, jnp.zeros((1, channels), extended.dtype)], axis=0)
    results = []
    for block_index in range(out_rows // taps):
        first = block_index * taps
        sources = extended[first : first + span].reshape(span, groups, width)
        limits = reach_back[first : first + taps]
        valid = (lag_table <= limits[:, None])[None]
        kernel_upper = jnp.where(valid, upper_part, zero_half)
        kernel_lower = jnp.where(valid, lower_part, zero_half)
        result = lax.dot_general(sources, kernel_upper, numbers, preferred_element_type=jnp.float32)
        result = result + lax.dot_general(
            sources, kernel_lower, numbers, preferred_element_type=jnp.float32
        )
        results.append(result.transpose(2, 0, 1).reshape(taps, channels))
    return jnp.concatenate(results, axis=0)


def tp_sum(value):
    count = lax.axis_size("tp")
    stride = 1
    while stride < count:
        value = value + lax.ppermute(value, "tp", [(i, i ^ stride) for i in range(count)])
        stride *= 2
    return value


def attend_block(queries, keys, values, visible, scale):
    head_count = queries.shape[1] // HEAD_DIM
    query_heads = queries.reshape(queries.shape[0], head_count, HEAD_DIM)
    key_heads = keys.reshape(keys.shape[0], head_count, HEAD_DIM)
    value_heads = values.reshape(values.shape[0], head_count, HEAD_DIM)
    scores = (
        jnp.einsum("qhd,khd->hqk", query_heads, key_heads, preferred_element_type=jnp.float32)
        * scale
    )
    scores = jnp.where(visible[None], scores, jnp.float32(-1e30))
    top = jnp.max(scores, axis=2, keepdims=True)
    expo = jnp.where(visible[None], jnp.exp(scores - top), jnp.float32(0.0))
    denominator = jnp.sum(expo, axis=2)
    summed = jnp.einsum(
        "hqk,khd->qhd", expo.astype(jnp.bfloat16), value_heads, preferred_element_type=jnp.float32
    )
    return summed, top[:, :, 0].T, denominator.T


def on_device(
    residual,
    hyena_gate,
    hyena_key,
    hyena_value,
    filter_taps,
    norm_gain,
    att_query,
    att_key,
    att_value,
    doc_lengths,
):
    tok_rows = residual.shape[0]
    taps = filter_taps.shape[1]
    shard_index = lax.axis_index("ctx")
    anchor = shard_index * tok_rows
    positions = anchor + jnp.arange(tok_rows, dtype=jnp.int32)
    doc_begin = document_begin(doc_lengths, positions)
    mixed_rows = (hyena_key.astype(jnp.float32) * hyena_value.astype(jnp.float32)).astype(
        jnp.bfloat16
    )
    rim_rows = shifted(mixed_rows[tok_rows - (taps - 1) :], "ctx", 1)
    key_pair = jnp.stack([att_key, att_value])
    previous = shifted(key_pair, "ctx", 1)
    later_query = shifted(att_query, "ctx", -2)
    key_rows = jnp.concatenate([previous[0], att_key], axis=0)
    value_rows = jnp.concatenate([previous[1], att_value], axis=0)
    window = key_rows.shape[0]
    key_pos = anchor - tok_rows + jnp.arange(window, dtype=jnp.int32)
    scale = jnp.float32(1.0 / HEAD_DIM**0.5)
    extended = jnp.concatenate([rim_rows, mixed_rows], axis=0)
    filtered = causal_filter(extended, filter_taps, positions - doc_begin, tok_rows)
    hidden = residual.astype(jnp.float32) + hyena_gate.astype(jnp.float32) * filtered
    local_sum = jnp.sum(hidden * hidden, axis=1)
    local_sum, later_query = lax.optimization_barrier((local_sum, later_query))
    far_pos = positions + 2 * tok_rows
    far_begin = document_begin(doc_lengths, far_pos)
    far_visible = (key_pos[None, :] <= far_pos[:, None]) & (key_pos[None, :] >= far_begin[:, None])
    far_sum, far_top, far_den = attend_block(later_query, key_rows, value_rows, far_visible, scale)
    far_stats = jnp.concatenate([far_top, far_den], axis=1)
    stat_cols = far_stats.shape[1]
    stat_high = far_stats.astype(jnp.bfloat16)
    stat_rest = far_stats - stat_high.astype(jnp.float32)
    stat_mid = stat_rest.astype(jnp.bfloat16)
    stat_low = (stat_rest - stat_mid.astype(jnp.float32)).astype(jnp.bfloat16)
    stat_pad = jnp.zeros((tok_rows, 128 - 3 * stat_cols), jnp.bfloat16)
    far_packet = jnp.concatenate(
        [far_sum.astype(jnp.bfloat16).reshape(tok_rows, -1), stat_high, stat_mid, stat_low, stat_pad],
        axis=1,
    )
    far_packet, local_sum, near_query = lax.optimization_barrier((far_packet, local_sum, att_query))
    far_packet = shifted(far_packet, "ctx", 2)
    sum_cols = far_sum.shape[1] * far_sum.shape[2]
    far_sum = far_packet[:, :sum_cols].reshape(far_sum.shape)
    stat_parts = far_packet[:, sum_cols : sum_cols + 3 * stat_cols].astype(jnp.float32)
    far_stats = stat_parts[:, :stat_cols] + (
        stat_parts[:, stat_cols : 2 * stat_cols] + stat_parts[:, 2 * stat_cols :]
    )
    mean_square = tp_sum(local_sum) / D
    normed = (hidden * lax.rsqrt(mean_square + norm_epsilon)[:, None] * norm_gain[None, :]).astype(
        jnp.bfloat16
    )
    head_count = far_top.shape[1]
    far_top, far_den = far_stats[:, :head_count], far_stats[:, head_count:]
    visible = (key_pos[None, :] <= positions[:, None]) & (key_pos[None, :] >= doc_begin[:, None])
    near_sum, near_top, near_den = attend_block(near_query, key_rows, value_rows, visible, scale)
    far_top = jnp.where(far_den > 0, far_top, jnp.float32(-1e30))
    top = jnp.maximum(near_top, far_top)
    near_scale = jnp.exp(near_top - top)
    far_scale = jnp.exp(far_top - top)
    denominator = near_den * near_scale + far_den * far_scale
    summed = near_sum * near_scale[:, :, None] + far_sum.astype(jnp.float32) * far_scale[:, :, None]
    attended = (summed / denominator[:, :, None]).astype(jnp.bfloat16).reshape(tok_rows, -1)
    return (normed, attended)


def solution(mesh):
    placed = (
        P("ctx", "tp"),
        P("ctx", "tp"),
        P("ctx", "tp"),
        P("ctx", "tp"),
        P("tp", None),
        P("tp"),
        P("ctx", "tp"),
        P("ctx", "tp"),
        P("ctx", "tp"),
        P(),
    )
    return jax.shard_map(
        on_device,
        mesh=mesh,
        in_specs=placed,
        out_specs=(P("ctx", "tp"), P("ctx", "tp")),
        check_vma=False,
    )
```

```python
import jax
import jax.numpy as jnp
from jax import lax
from jax.experimental import pallas as pl
from jax.experimental.pallas import tpu as pltpu
from jax.sharding import PartitionSpec as P

D = 8192
HEAD_DIM = 128
REACH = 3


norm_epsilon = 1e-05


def shifted(value, axis, steps):
    count = lax.axis_size(axis)
    first, last = (max(0, -steps), min(count, count - steps))
    return lax.ppermute(value, axis, [(source, source + steps) for source in range(first, last)])


def document_begin(doc_lengths, positions):
    count = doc_lengths.shape[0]
    order = jnp.arange(count, dtype=jnp.int32)
    before = order[None, :] < order[:, None]
    starts = jnp.sum(jnp.where(before, doc_lengths[None, :], 0), axis=1)
    return jnp.max(jnp.where(starts[None, :] <= positions[:, None], starts[None, :], 0), axis=1)


def toeplitz_rows(reversed_ref, out_ref):
    rows = out_ref.shape[1]
    for group in range(out_ref.shape[0]):
        line = jnp.broadcast_to(reversed_ref[group : group + 1, :], (rows, reversed_ref.shape[1]))
        out_ref[group] = pltpu.roll(line, 0, 1, stride=1, stride_axis=0)


def build_toeplitz(filter_taps):
    groups, taps = filter_taps.shape
    span = 2 * taps
    reversed_taps = jnp.concatenate(
        [filter_taps[:, ::-1], jnp.zeros((groups, span - taps), jnp.float32)], axis=1
    )
    step = 8
    return pl.pallas_call(
        toeplitz_rows,
        grid=(groups // step,),
        in_specs=[pl.BlockSpec((step, span), lambda i: (i, 0))],
        out_specs=pl.BlockSpec((step, taps, span), lambda i: (i, 0, 0)),
        out_shape=jax.ShapeDtypeStruct((groups, taps, span), jnp.float32),
    )(reversed_taps)


def causal_filter(extended, filter_taps, reach_back, out_rows, between):
    groups, taps = filter_taps.shape
    channels = extended.shape[1]
    width = channels // groups
    span = 2 * taps
    lag_table = (
        jnp.arange(taps, dtype=jnp.int32)[:, None]
        + (taps - 1)
        - jnp.arange(span, dtype=jnp.int32)[None, :]
    )
    toeplitz = build_toeplitz(filter_taps)
    upper_part = toeplitz.astype(jnp.bfloat16)
    lower_part = (toeplitz - upper_part.astype(jnp.float32)).astype(jnp.bfloat16)
    zero_half = jnp.zeros((), jnp.bfloat16)
    numbers = (((0,), (2,)), ((1,), (0,)))
    extended = jnp.concatenate([extended, jnp.zeros((1, channels), extended.dtype)], axis=0)
    results = []
    for block_index in range(out_rows // taps):
        if block_index == 1:
            extended = between(results[0], extended)
        first = block_index * taps
        sources = extended[first : first + span].reshape(span, groups, width)
        limits = reach_back[first : first + taps]
        valid = (lag_table <= limits[:, None])[None]
        kernel_upper = jnp.where(valid, upper_part, zero_half)
        kernel_lower = jnp.where(valid, lower_part, zero_half)
        result = lax.dot_general(sources, kernel_upper, numbers, preferred_element_type=jnp.float32)
        result = result + lax.dot_general(
            sources, kernel_lower, numbers, preferred_element_type=jnp.float32
        )
        results.append(result.transpose(2, 0, 1).reshape(taps, channels))
    return jnp.concatenate(results, axis=0)


def tp_sum(value):
    count = lax.axis_size("tp")
    stride = 1
    while stride < count:
        value = value + lax.ppermute(value, "tp", [(i, i ^ stride) for i in range(count)])
        stride *= 2
    return value


def attend_block(queries, keys, values, visible, scale):
    head_count = queries.shape[1] // HEAD_DIM
    query_heads = queries.reshape(queries.shape[0], head_count, HEAD_DIM)
    key_heads = keys.reshape(keys.shape[0], head_count, HEAD_DIM)
    value_heads = values.reshape(values.shape[0], head_count, HEAD_DIM)
    scores = (
        jnp.einsum("qhd,khd->hqk", query_heads, key_heads, preferred_element_type=jnp.float32)
        * scale
    )
    scores = jnp.where(visible[None], scores, jnp.float32(-1e30))
    top = jnp.max(scores, axis=2, keepdims=True)
    expo = jnp.where(visible[None], jnp.exp(scores - top), jnp.float32(0.0))
    denominator = jnp.sum(expo, axis=2)
    summed = jnp.einsum(
        "hqk,khd->qhd", expo.astype(jnp.bfloat16), value_heads, preferred_element_type=jnp.float32
    )
    return summed, top[:, :, 0].T, denominator.T


def on_device(
    residual,
    hyena_gate,
    hyena_key,
    hyena_value,
    filter_taps,
    norm_gain,
    att_query,
    att_key,
    att_value,
    doc_lengths,
):
    tok_rows = residual.shape[0]
    taps = filter_taps.shape[1]
    shard_index = lax.axis_index("ctx")
    anchor = shard_index * tok_rows
    positions = anchor + jnp.arange(tok_rows, dtype=jnp.int32)
    doc_begin = document_begin(doc_lengths, positions)
    mixed_rows = (hyena_key.astype(jnp.float32) * hyena_value.astype(jnp.float32)).astype(
        jnp.bfloat16
    )
    rim_rows = shifted(mixed_rows[tok_rows - (taps - 1) :], "ctx", 1)
    key_pair = jnp.stack([att_key, att_value])
    previous = shifted(key_pair, "ctx", 1)
    later_query = shifted(att_query, "ctx", -2)
    key_rows = jnp.concatenate([previous[0], att_key], axis=0)
    value_rows = jnp.concatenate([previous[1], att_value], axis=0)
    window = key_rows.shape[0]
    key_pos = anchor - tok_rows + jnp.arange(window, dtype=jnp.int32)
    scale = jnp.float32(1.0 / HEAD_DIM**0.5)
    far_pos = positions + 2 * tok_rows
    far_begin = document_begin(doc_lengths, far_pos)
    far_visible = (key_pos[None, :] <= far_pos[:, None]) & (key_pos[None, :] >= far_begin[:, None])
    held = {}

    def far_part(first_rows, extended):
        first_rows, queries = lax.optimization_barrier((first_rows, later_query))
        far_sum, far_top, far_den = attend_block(queries, key_rows, value_rows, far_visible, scale)
        far_stats = jnp.concatenate([far_top, far_den], axis=1)
        stat_cols = far_stats.shape[1]
        stat_high = far_stats.astype(jnp.bfloat16)
        stat_rest = far_stats - stat_high.astype(jnp.float32)
        stat_mid = stat_rest.astype(jnp.bfloat16)
        stat_low = (stat_rest - stat_mid.astype(jnp.float32)).astype(jnp.bfloat16)
        stat_pad = jnp.zeros((tok_rows, 128 - 3 * stat_cols), jnp.bfloat16)
        far_packet = jnp.concatenate(
            [far_sum.astype(jnp.bfloat16).reshape(tok_rows, -1), stat_high, stat_mid, stat_low, stat_pad],
            axis=1,
        )
        far_packet, extended, held["query"] = lax.optimization_barrier(
            (far_packet, extended, att_query)
        )
        held["packet"] = shifted(far_packet, "ctx", 2)
        held["shape"] = far_sum.shape
        held["stat_cols"] = stat_cols
        return extended

    extended = jnp.concatenate([rim_rows, mixed_rows], axis=0)
    filtered = causal_filter(extended, filter_taps, positions - doc_begin, tok_rows, far_part)
    hidden = residual.astype(jnp.float32) + hyena_gate.astype(jnp.float32) * filtered
    local_sum = jnp.sum(hidden * hidden, axis=1)
    mean_square = tp_sum(local_sum) / D
    normed = (hidden * lax.rsqrt(mean_square + norm_epsilon)[:, None] * norm_gain[None, :]).astype(
        jnp.bfloat16
    )
    far_packet, near_query, stat_cols = held["packet"], held["query"], held["stat_cols"]
    sum_shape = held["shape"]
    sum_cols = sum_shape[1] * sum_shape[2]
    far_sum = far_packet[:, :sum_cols].reshape(sum_shape)
    stat_parts = far_packet[:, sum_cols : sum_cols + 3 * stat_cols].astype(jnp.float32)
    far_stats = stat_parts[:, :stat_cols] + (
        stat_parts[:, stat_cols : 2 * stat_cols] + stat_parts[:, 2 * stat_cols :]
    )
    head_count = sum_shape[1]
    far_top, far_den = far_stats[:, :head_count], far_stats[:, head_count:]
    visible = (key_pos[None, :] <= positions[:, None]) & (key_pos[None, :] >= doc_begin[:, None])
    near_sum, near_top, near_den = attend_block(near_query, key_rows, value_rows, visible, scale)
    far_top = jnp.where(far_den > 0, far_top, jnp.float32(-1e30))
    top = jnp.maximum(near_top, far_top)
    near_scale = jnp.exp(near_top - top)
    far_scale = jnp.exp(far_top - top)
    denominator = near_den * near_scale + far_den * far_scale
    summed = near_sum * near_scale[:, :, None] + far_sum.astype(jnp.float32) * far_scale[:, :, None]
    attended = (summed / denominator[:, :, None]).astype(jnp.bfloat16).reshape(tok_rows, -1)
    return (normed, attended)


def solution(mesh):
    placed = (
        P("ctx", "tp"),
        P("ctx", "tp"),
        P("ctx", "tp"),
        P("ctx", "tp"),
        P("tp", None),
        P("tp"),
        P("ctx", "tp"),
        P("ctx", "tp"),
        P("ctx", "tp"),
        P(),
    )
    return jax.shard_map(
        on_device,
        mesh=mesh,
        in_specs=placed,
        out_specs=(P("ctx", "tp"), P("ctx", "tp")),
        check_vma=False,
    )
```

```python
import jax
import jax.numpy as jnp
from jax import lax
from jax.experimental import pallas as pl
from jax.experimental.pallas import tpu as pltpu
from jax.sharding import PartitionSpec as P

D = 8192
HEAD_DIM = 128


norm_epsilon = 1e-05


def shifted(value, axis, steps):
    count = lax.axis_size(axis)
    first, last = (max(0, -steps), min(count, count - steps))
    return lax.ppermute(value, axis, [(source, source + steps) for source in range(first, last)])


def document_begin(doc_lengths, positions):
    count = doc_lengths.shape[0]
    order = jnp.arange(count, dtype=jnp.int32)
    before = order[None, :] < order[:, None]
    starts = jnp.sum(jnp.where(before, doc_lengths[None, :], 0), axis=1)
    return jnp.max(jnp.where(starts[None, :] <= positions[:, None], starts[None, :], 0), axis=1)


def toeplitz_rows(reversed_ref, out_ref):
    rows = out_ref.shape[1]
    for group in range(out_ref.shape[0]):
        line = jnp.broadcast_to(reversed_ref[group : group + 1, :], (rows, reversed_ref.shape[1]))
        out_ref[group] = pltpu.roll(line, 0, 1, stride=1, stride_axis=0)


def build_toeplitz(filter_taps):
    groups, taps = filter_taps.shape
    span = 2 * taps
    reversed_taps = jnp.concatenate(
        [filter_taps[:, ::-1], jnp.zeros((groups, span - taps), jnp.float32)], axis=1
    )
    step = 8
    return pl.pallas_call(
        toeplitz_rows,
        grid=(groups // step,),
        in_specs=[pl.BlockSpec((step, span), lambda i: (i, 0))],
        out_specs=pl.BlockSpec((step, taps, span), lambda i: (i, 0, 0)),
        out_shape=jax.ShapeDtypeStruct((groups, taps, span), jnp.float32),
    )(reversed_taps)


def causal_filter(extended, filter_taps, reach_back, out_rows, between):
    groups, taps = filter_taps.shape
    channels = extended.shape[1]
    width = channels // groups
    span = 2 * taps
    lag_table = (
        jnp.arange(taps, dtype=jnp.int32)[:, None]
        + (taps - 1)
        - jnp.arange(span, dtype=jnp.int32)[None, :]
    )
    toeplitz = build_toeplitz(filter_taps)
    upper_part = toeplitz.astype(jnp.bfloat16)
    lower_part = (toeplitz - upper_part.astype(jnp.float32)).astype(jnp.bfloat16)
    zero_half = jnp.zeros((), jnp.bfloat16)
    numbers = (((0,), (2,)), ((1,), (0,)))
    extended = jnp.concatenate([extended, jnp.zeros((1, channels), extended.dtype)], axis=0)
    results = []
    for block_index in range(out_rows // taps):
        if block_index == 1:
            extended = between(results[0], extended)
        first = block_index * taps
        sources = extended[first : first + span].reshape(span, groups, width)
        limits = reach_back[first : first + taps]
        valid = (lag_table <= limits[:, None])[None]
        kernel_upper = jnp.where(valid, upper_part, zero_half)
        kernel_lower = jnp.where(valid, lower_part, zero_half)
        result = lax.dot_general(sources, kernel_upper, numbers, preferred_element_type=jnp.float32)
        result = result + lax.dot_general(
            sources, kernel_lower, numbers, preferred_element_type=jnp.float32
        )
        results.append(result.transpose(2, 0, 1).reshape(taps, channels))
    return jnp.concatenate(results, axis=0)


def tp_sum(value):
    count = lax.axis_size("tp")
    stride = 1
    while stride < count:
        value = value + lax.ppermute(value, "tp", [(i, i ^ stride) for i in range(count)])
        stride *= 2
    return value


def attend_block(queries, keys, values, visible, scale):
    head_count = queries.shape[1] // HEAD_DIM
    query_heads = queries.reshape(queries.shape[0], head_count, HEAD_DIM)
    key_heads = keys.reshape(keys.shape[0], head_count, HEAD_DIM)
    value_heads = values.reshape(values.shape[0], head_count, HEAD_DIM)
    scores = (
        jnp.einsum("qhd,khd->hqk", query_heads, key_heads, preferred_element_type=jnp.float32)
        * scale
    )
    scores = jnp.where(visible[None], scores, jnp.float32(-1e30))
    top = jnp.max(scores, axis=2, keepdims=True)
    expo = jnp.where(visible[None], jnp.exp(scores - top), jnp.float32(0.0))
    denominator = jnp.sum(expo, axis=2)
    summed = jnp.einsum(
        "hqk,khd->qhd", expo.astype(jnp.bfloat16), value_heads, preferred_element_type=jnp.float32
    )
    return summed, top[:, :, 0].T, denominator.T


def block_body(
    residual,
    hyena_gate,
    hyena_key,
    hyena_value,
    filter_taps,
    norm_gain,
    att_query,
    att_key,
    att_value,
    doc_lengths,
):
    tok_rows = residual.shape[0]
    taps = filter_taps.shape[1]
    shard_index = lax.axis_index("ctx")
    anchor = shard_index * tok_rows
    positions = anchor + jnp.arange(tok_rows, dtype=jnp.int32)
    doc_begin = document_begin(doc_lengths, positions)
    mixed_rows = (hyena_key.astype(jnp.float32) * hyena_value.astype(jnp.float32)).astype(
        jnp.bfloat16
    )
    rim_rows = shifted(mixed_rows[tok_rows - (taps - 1) :], "ctx", 1)
    key_pair = jnp.stack([att_key, att_value])
    previous = shifted(key_pair, "ctx", 1)
    later_query = shifted(att_query, "ctx", -2)
    key_rows = jnp.concatenate([previous[0], att_key], axis=0)
    value_rows = jnp.concatenate([previous[1], att_value], axis=0)
    window = key_rows.shape[0]
    key_pos = anchor - tok_rows + jnp.arange(window, dtype=jnp.int32)
    scale = jnp.float32(1.0 / HEAD_DIM**0.5)
    far_pos = positions + 2 * tok_rows
    far_begin = document_begin(doc_lengths, far_pos)
    far_visible = (key_pos[None, :] <= far_pos[:, None]) & (key_pos[None, :] >= far_begin[:, None])
    held = {}

    def far_part(first_rows, extended):
        first_rows, queries = lax.optimization_barrier((first_rows, later_query))
        far_sum, far_top, far_den = attend_block(queries, key_rows, value_rows, far_visible, scale)
        far_stats = jnp.concatenate([far_top, far_den], axis=1)
        stat_cols = far_stats.shape[1]
        stat_high = far_stats.astype(jnp.bfloat16)
        stat_rest = far_stats - stat_high.astype(jnp.float32)
        stat_mid = stat_rest.astype(jnp.bfloat16)
        stat_low = (stat_rest - stat_mid.astype(jnp.float32)).astype(jnp.bfloat16)
        stat_pad = jnp.zeros((tok_rows, 128 - 3 * stat_cols), jnp.bfloat16)
        far_packet = jnp.concatenate(
            [far_sum.astype(jnp.bfloat16).reshape(tok_rows, -1), stat_high, stat_mid, stat_low, stat_pad],
            axis=1,
        )
        far_packet, extended, held["query"] = lax.optimization_barrier(
            (far_packet, extended, att_query)
        )
        held["packet"] = shifted(far_packet, "ctx", 2)
        held["shape"] = far_sum.shape
        held["stat_cols"] = stat_cols
        return extended

    extended = jnp.concatenate([rim_rows, mixed_rows], axis=0)
    filtered = causal_filter(extended, filter_taps, positions - doc_begin, tok_rows, far_part)
    hidden = residual.astype(jnp.float32) + hyena_gate.astype(jnp.float32) * filtered
    local_sum = jnp.sum(hidden * hidden, axis=1)
    mean_square = tp_sum(local_sum) / D
    normed = (hidden * lax.rsqrt(mean_square + norm_epsilon)[:, None] * norm_gain[None, :]).astype(
        jnp.bfloat16
    )
    far_packet, near_query, stat_cols = held["packet"], held["query"], held["stat_cols"]
    sum_shape = held["shape"]
    sum_cols = sum_shape[1] * sum_shape[2]
    far_sum = far_packet[:, :sum_cols].reshape(sum_shape)
    stat_parts = far_packet[:, sum_cols : sum_cols + 3 * stat_cols].astype(jnp.float32)
    far_stats = stat_parts[:, :stat_cols] + (
        stat_parts[:, stat_cols : 2 * stat_cols] + stat_parts[:, 2 * stat_cols :]
    )
    head_count = sum_shape[1]
    far_top, far_den = far_stats[:, :head_count], far_stats[:, head_count:]
    visible = (key_pos[None, :] <= positions[:, None]) & (key_pos[None, :] >= doc_begin[:, None])
    near_sum, near_top, near_den = attend_block(near_query, key_rows, value_rows, visible, scale)
    far_top = jnp.where(far_den > 0, far_top, jnp.float32(-1e30))
    top = jnp.maximum(near_top, far_top)
    near_scale = jnp.exp(near_top - top)
    far_scale = jnp.exp(far_top - top)
    denominator = near_den * near_scale + far_den * far_scale
    summed = near_sum * near_scale[:, :, None] + far_sum.astype(jnp.float32) * far_scale[:, :, None]
    attended = (summed / denominator[:, :, None]).astype(jnp.bfloat16).reshape(tok_rows, -1)
    return (normed, attended)


def solution(mesh):
    placed = (
        P("ctx", "tp"),
        P("ctx", "tp"),
        P("ctx", "tp"),
        P("ctx", "tp"),
        P("tp", None),
        P("tp"),
        P("ctx", "tp"),
        P("ctx", "tp"),
        P("ctx", "tp"),
        P(),
    )
    return jax.shard_map(
        block_body,
        mesh=mesh,
        in_specs=placed,
        out_specs=(P("ctx", "tp"), P("ctx", "tp")),
        check_vma=False,
    )
```

```python
import jax
import jax.numpy as jnp
from jax import lax
from jax.experimental import pallas as pl
from jax.experimental.pallas import tpu as pltpu
from jax.sharding import PartitionSpec as P

D = 8192
HEAD_DIM = 128


norm_epsilon = 1e-05


def shifted(value, axis, steps):
    count = lax.axis_size(axis)
    first, last = (max(0, -steps), min(count, count - steps))
    return lax.ppermute(value, axis, [(source, source + steps) for source in range(first, last)])


def document_begin(doc_lengths, positions):
    count = doc_lengths.shape[0]
    order = jnp.arange(count, dtype=jnp.int32)
    before = order[None, :] < order[:, None]
    starts = jnp.sum(jnp.where(before, doc_lengths[None, :], 0), axis=1)
    return jnp.max(jnp.where(starts[None, :] <= positions[:, None], starts[None, :], 0), axis=1)


def toeplitz_rows(reversed_ref, out_ref):
    rows = out_ref.shape[1]
    for group in range(out_ref.shape[0]):
        line = jnp.broadcast_to(reversed_ref[group : group + 1, :], (rows, reversed_ref.shape[1]))
        out_ref[group] = pltpu.roll(line, 0, 1, stride=1, stride_axis=0)


def build_toeplitz(filter_taps):
    groups, taps = filter_taps.shape
    span = 2 * taps
    reversed_taps = jnp.concatenate(
        [filter_taps[:, ::-1], jnp.zeros((groups, span - taps), jnp.float32)], axis=1
    )
    step = 8
    return pl.pallas_call(
        toeplitz_rows,
        grid=(groups // step,),
        in_specs=[pl.BlockSpec((step, span), lambda i: (i, 0))],
        out_specs=pl.BlockSpec((step, taps, span), lambda i: (i, 0, 0)),
        out_shape=jax.ShapeDtypeStruct((groups, taps, span), jnp.float32),
    )(reversed_taps)


def causal_filter(extended, filter_taps, reach_back, out_rows, between):
    groups, taps = filter_taps.shape
    channels = extended.shape[1]
    width = channels // groups
    span = 2 * taps
    lag_table = (
        jnp.arange(taps, dtype=jnp.int32)[:, None]
        + (taps - 1)
        - jnp.arange(span, dtype=jnp.int32)[None, :]
    )
    toeplitz = build_toeplitz(filter_taps)
    upper_part = toeplitz.astype(jnp.bfloat16)
    lower_part = (toeplitz - upper_part.astype(jnp.float32)).astype(jnp.bfloat16)
    zero_half = jnp.zeros((), jnp.bfloat16)
    numbers = (((0,), (2,)), ((1,), (0,)))
    extended = jnp.concatenate([extended, jnp.zeros((1, channels), extended.dtype)], axis=0)
    results = []
    for block_index in range(out_rows // taps):
        if block_index == 1:
            extended = between(results[0], extended)
        first = block_index * taps
        sources = extended[first : first + span].reshape(span, groups, width)
        limits = reach_back[first : first + taps]
        valid = (lag_table <= limits[:, None])[None]
        kernel_upper = jnp.where(valid, upper_part, zero_half)
        kernel_lower = jnp.where(valid, lower_part, zero_half)
        result = lax.dot_general(sources, kernel_upper, numbers, preferred_element_type=jnp.float32)
        result = result + lax.dot_general(
            sources, kernel_lower, numbers, preferred_element_type=jnp.float32
        )
        results.append(result.transpose(2, 0, 1).reshape(taps, channels))
    return jnp.concatenate(results, axis=0)


def tp_sum(value):
    count = lax.axis_size("tp")
    stride = 1
    while stride < count:
        value = value + lax.ppermute(value, "tp", [(i, i ^ stride) for i in range(count)])
        stride *= 2
    return value


def attend_block(queries, keys, values, visible, scale):
    head_count = queries.shape[1] // HEAD_DIM
    query_heads = queries.reshape(queries.shape[0], head_count, HEAD_DIM)
    key_heads = keys.reshape(keys.shape[0], head_count, HEAD_DIM)
    value_heads = values.reshape(values.shape[0], head_count, HEAD_DIM)
    scores = (
        jnp.einsum("qhd,khd->hqk", query_heads, key_heads, preferred_element_type=jnp.float32)
        * scale
    )
    scores = jnp.where(visible[None], scores, jnp.float32(-1e30))
    top = jnp.max(scores, axis=2, keepdims=True)
    expo = jnp.where(visible[None], jnp.exp(scores - top), jnp.float32(0.0))
    denominator = jnp.sum(expo, axis=2)
    summed = jnp.einsum(
        "hqk,khd->qhd", expo.astype(jnp.bfloat16), value_heads, preferred_element_type=jnp.float32
    )
    return summed, top[:, :, 0].T, denominator.T


def block_body(
    residual,
    hyena_gate,
    hyena_key,
    hyena_value,
    filter_taps,
    norm_gain,
    att_query,
    att_key,
    att_value,
    doc_lengths,
):
    tok_rows = residual.shape[0]
    taps = filter_taps.shape[1]
    shard_index = lax.axis_index("ctx")
    anchor = shard_index * tok_rows
    positions = anchor + jnp.arange(tok_rows, dtype=jnp.int32)
    doc_begin = document_begin(doc_lengths, positions)
    mixed_rows = (hyena_key.astype(jnp.float32) * hyena_value.astype(jnp.float32)).astype(
        jnp.bfloat16
    )
    rim_rows = shifted(mixed_rows[tok_rows - (taps - 1) :], "ctx", 1)
    key_pair = jnp.stack([att_key, att_value])
    previous = shifted(key_pair, "ctx", 1)
    later_query = shifted(att_query, "ctx", -2)
    key_rows = jnp.concatenate([previous[0], att_key], axis=0)
    value_rows = jnp.concatenate([previous[1], att_value], axis=0)
    window = key_rows.shape[0]
    key_pos = anchor - tok_rows + jnp.arange(window, dtype=jnp.int32)
    scale = jnp.float32(1.0 / HEAD_DIM**0.5)
    far_pos = positions + 2 * tok_rows
    far_begin = document_begin(doc_lengths, far_pos)
    far_visible = (key_pos[None, :] <= far_pos[:, None]) & (key_pos[None, :] >= far_begin[:, None])
    held = {}
    visible = (key_pos[None, :] <= positions[:, None]) & (key_pos[None, :] >= doc_begin[:, None])
    near_sum, near_top, near_den = attend_block(att_query, key_rows, value_rows, visible, scale)

    def far_part(first_rows, extended):
        first_rows, queries, held["near"] = lax.optimization_barrier(
            (first_rows, later_query, (near_sum, near_top, near_den))
        )
        far_sum, far_top, far_den = attend_block(queries, key_rows, value_rows, far_visible, scale)
        far_stats = jnp.concatenate([far_top, far_den], axis=1)
        stat_cols = far_stats.shape[1]
        stat_high = far_stats.astype(jnp.bfloat16)
        stat_rest = far_stats - stat_high.astype(jnp.float32)
        stat_mid = stat_rest.astype(jnp.bfloat16)
        stat_low = (stat_rest - stat_mid.astype(jnp.float32)).astype(jnp.bfloat16)
        stat_pad = jnp.zeros((tok_rows, 128 - 3 * stat_cols), jnp.bfloat16)
        far_packet = jnp.concatenate(
            [far_sum.astype(jnp.bfloat16).reshape(tok_rows, -1), stat_high, stat_mid, stat_low, stat_pad],
            axis=1,
        )
        far_packet, extended = lax.optimization_barrier((far_packet, extended))
        held["packet"] = shifted(far_packet, "ctx", 2)
        held["shape"] = far_sum.shape
        held["stat_cols"] = stat_cols
        return extended

    extended = jnp.concatenate([rim_rows, mixed_rows], axis=0)
    filtered = causal_filter(extended, filter_taps, positions - doc_begin, tok_rows, far_part)
    hidden = residual.astype(jnp.float32) + hyena_gate.astype(jnp.float32) * filtered
    local_sum = jnp.sum(hidden * hidden, axis=1)
    mean_square = tp_sum(local_sum) / D
    normed = (hidden * lax.rsqrt(mean_square + norm_epsilon)[:, None] * norm_gain[None, :]).astype(
        jnp.bfloat16
    )
    far_packet, stat_cols = held["packet"], held["stat_cols"]
    near_sum, near_top, near_den = held["near"]
    sum_shape = held["shape"]
    sum_cols = sum_shape[1] * sum_shape[2]
    far_sum = far_packet[:, :sum_cols].reshape(sum_shape)
    stat_parts = far_packet[:, sum_cols : sum_cols + 3 * stat_cols].astype(jnp.float32)
    far_stats = stat_parts[:, :stat_cols] + (
        stat_parts[:, stat_cols : 2 * stat_cols] + stat_parts[:, 2 * stat_cols :]
    )
    head_count = sum_shape[1]
    far_top, far_den = far_stats[:, :head_count], far_stats[:, head_count:]
    far_top = jnp.where(far_den > 0, far_top, jnp.float32(-1e30))
    top = jnp.maximum(near_top, far_top)
    near_scale = jnp.exp(near_top - top)
    far_scale = jnp.exp(far_top - top)
    denominator = near_den * near_scale + far_den * far_scale
    summed = near_sum * near_scale[:, :, None] + far_sum.astype(jnp.float32) * far_scale[:, :, None]
    attended = (summed / denominator[:, :, None]).astype(jnp.bfloat16).reshape(tok_rows, -1)
    return (normed, attended)


def solution(mesh):
    placed = (
        P("ctx", "tp"),
        P("ctx", "tp"),
        P("ctx", "tp"),
        P("ctx", "tp"),
        P("tp", None),
        P("tp"),
        P("ctx", "tp"),
        P("ctx", "tp"),
        P("ctx", "tp"),
        P(),
    )
    return jax.shard_map(
        block_body,
        mesh=mesh,
        in_specs=placed,
        out_specs=(P("ctx", "tp"), P("ctx", "tp")),
        check_vma=False,
    )
```

```python
import jax
import jax.numpy as jnp
from jax import lax
from jax.experimental import pallas as pl
from jax.experimental.pallas import tpu as pltpu
from jax.sharding import PartitionSpec as P

D = 8192
HEAD_DIM = 128


norm_epsilon = 1e-05


def shifted(value, axis, steps):
    count = lax.axis_size(axis)
    first, last = (max(0, -steps), min(count, count - steps))
    return lax.ppermute(value, axis, [(source, source + steps) for source in range(first, last)])


def document_begin(doc_lengths, positions):
    count = doc_lengths.shape[0]
    order = jnp.arange(count, dtype=jnp.int32)
    before = order[None, :] < order[:, None]
    starts = jnp.sum(jnp.where(before, doc_lengths[None, :], 0), axis=1)
    return jnp.max(jnp.where(starts[None, :] <= positions[:, None], starts[None, :], 0), axis=1)


def toeplitz_rows(reversed_ref, out_ref):
    rows = out_ref.shape[1]
    for group in range(out_ref.shape[0]):
        line = jnp.broadcast_to(reversed_ref[group : group + 1, :], (rows, reversed_ref.shape[1]))
        out_ref[group] = pltpu.roll(line, 0, 1, stride=1, stride_axis=0)


def build_toeplitz(filter_taps):
    groups, taps = filter_taps.shape
    span = 2 * taps
    reversed_taps = jnp.concatenate(
        [filter_taps[:, ::-1], jnp.zeros((groups, span - taps), jnp.float32)], axis=1
    )
    step = 8
    return pl.pallas_call(
        toeplitz_rows,
        grid=(groups // step,),
        in_specs=[pl.BlockSpec((step, span), lambda i: (i, 0))],
        out_specs=pl.BlockSpec((step, taps, span), lambda i: (i, 0, 0)),
        out_shape=jax.ShapeDtypeStruct((groups, taps, span), jnp.float32),
    )(reversed_taps)


def causal_filter(mixed_rows, rim_rows, filter_taps, reach_back, out_rows, between):
    groups, taps = filter_taps.shape
    channels = mixed_rows.shape[1]
    width = channels // groups
    span = 2 * taps
    lag_table = (
        jnp.arange(taps, dtype=jnp.int32)[:, None]
        + (taps - 1)
        - jnp.arange(span, dtype=jnp.int32)[None, :]
    )
    toeplitz = build_toeplitz(filter_taps)
    upper_part = toeplitz.astype(jnp.bfloat16)
    lower_part = (toeplitz - upper_part.astype(jnp.float32)).astype(jnp.bfloat16)
    zero_half = jnp.zeros((), jnp.bfloat16)
    numbers = (((0,), (2,)), ((1,), (0,)))
    padded = jnp.concatenate([mixed_rows, jnp.zeros((1, channels), mixed_rows.dtype)], axis=0)
    block_count = out_rows // taps
    results = [None] * block_count
    for step, block_index in enumerate(range(block_count - 1, -1, -1)):
        if step == 1:
            rim_rows, padded = between(results[block_count - 1], (rim_rows, padded))
        first = block_index * taps - (taps - 1)
        if first >= 0:
            sources = padded[first : first + span]
        else:
            sources = jnp.concatenate([rim_rows[first + taps - 1 :], padded[: first + span]], axis=0)
        sources = sources.reshape(span, groups, width)
        limits = reach_back[block_index * taps : (block_index + 1) * taps]
        valid = (lag_table <= limits[:, None])[None]
        kernel_upper = jnp.where(valid, upper_part, zero_half)
        kernel_lower = jnp.where(valid, lower_part, zero_half)
        result = lax.dot_general(sources, kernel_upper, numbers, preferred_element_type=jnp.float32)
        result = result + lax.dot_general(
            sources, kernel_lower, numbers, preferred_element_type=jnp.float32
        )
        results[block_index] = result.transpose(2, 0, 1).reshape(taps, channels)
    return jnp.concatenate(results, axis=0)


def tp_sum(value):
    count = lax.axis_size("tp")
    stride = 1
    while stride < count:
        value = value + lax.ppermute(value, "tp", [(i, i ^ stride) for i in range(count)])
        stride *= 2
    return value


def attend_block(queries, keys, values, visible, scale):
    head_count = queries.shape[1] // HEAD_DIM
    query_heads = queries.reshape(queries.shape[0], head_count, HEAD_DIM)
    key_heads = keys.reshape(keys.shape[0], head_count, HEAD_DIM)
    value_heads = values.reshape(values.shape[0], head_count, HEAD_DIM)
    scores = (
        jnp.einsum("qhd,khd->hqk", query_heads, key_heads, preferred_element_type=jnp.float32)
        * scale
    )
    scores = jnp.where(visible[None], scores, jnp.float32(-1e30))
    top = jnp.max(scores, axis=2, keepdims=True)
    expo = jnp.where(visible[None], jnp.exp(scores - top), jnp.float32(0.0))
    denominator = jnp.sum(expo, axis=2)
    summed = jnp.einsum(
        "hqk,khd->qhd", expo.astype(jnp.bfloat16), value_heads, preferred_element_type=jnp.float32
    )
    return summed, top[:, :, 0].T, denominator.T


def block_body(
    residual,
    hyena_gate,
    hyena_key,
    hyena_value,
    filter_taps,
    norm_gain,
    att_query,
    att_key,
    att_value,
    doc_lengths,
):
    tok_rows = residual.shape[0]
    taps = filter_taps.shape[1]
    shard_index = lax.axis_index("ctx")
    anchor = shard_index * tok_rows
    positions = anchor + jnp.arange(tok_rows, dtype=jnp.int32)
    doc_begin = document_begin(doc_lengths, positions)
    mixed_rows = (hyena_key.astype(jnp.float32) * hyena_value.astype(jnp.float32)).astype(
        jnp.bfloat16
    )
    packet = jnp.concatenate([att_key, att_value, mixed_rows[tok_rows - (taps - 1) :]], axis=0)
    received = shifted(packet, "ctx", 1)
    previous = (received[:tok_rows], received[tok_rows : 2 * tok_rows])
    rim_rows = received[2 * tok_rows :]
    later_query = shifted(att_query, "ctx", -2)
    key_rows = jnp.concatenate([previous[0], att_key], axis=0)
    value_rows = jnp.concatenate([previous[1], att_value], axis=0)
    window = key_rows.shape[0]
    key_pos = anchor - tok_rows + jnp.arange(window, dtype=jnp.int32)
    scale = jnp.float32(1.0 / HEAD_DIM**0.5)
    far_pos = positions + 2 * tok_rows
    far_begin = document_begin(doc_lengths, far_pos)
    far_visible = (key_pos[None, :] <= far_pos[:, None]) & (key_pos[None, :] >= far_begin[:, None])
    held = {}
    visible = (key_pos[None, :] <= positions[:, None]) & (key_pos[None, :] >= doc_begin[:, None])
    near_sum, near_top, near_den = attend_block(att_query, key_rows, value_rows, visible, scale)

    def far_part(first_rows, extended):
        first_rows, queries, held["near"] = lax.optimization_barrier(
            (first_rows, later_query, (near_sum, near_top, near_den))
        )
        far_sum, far_top, far_den = attend_block(queries, key_rows, value_rows, far_visible, scale)
        far_stats = jnp.concatenate([far_top, far_den], axis=1)
        stat_cols = far_stats.shape[1]
        stat_high = far_stats.astype(jnp.bfloat16)
        stat_rest = far_stats - stat_high.astype(jnp.float32)
        stat_mid = stat_rest.astype(jnp.bfloat16)
        stat_low = (stat_rest - stat_mid.astype(jnp.float32)).astype(jnp.bfloat16)
        stat_pad = jnp.zeros((tok_rows, 128 - 3 * stat_cols), jnp.bfloat16)
        far_packet = jnp.concatenate(
            [far_sum.astype(jnp.bfloat16).reshape(tok_rows, -1), stat_high, stat_mid, stat_low, stat_pad],
            axis=1,
        )
        far_packet, extended = lax.optimization_barrier((far_packet, extended))
        held["packet"] = shifted(far_packet, "ctx", 2)
        held["shape"] = far_sum.shape
        held["stat_cols"] = stat_cols
        return extended

    filtered = causal_filter(
        mixed_rows, rim_rows, filter_taps, positions - doc_begin, tok_rows, far_part
    )
    hidden = residual.astype(jnp.float32) + hyena_gate.astype(jnp.float32) * filtered
    local_sum = jnp.sum(hidden * hidden, axis=1)
    mean_square = tp_sum(local_sum) / D
    normed = (hidden * lax.rsqrt(mean_square + norm_epsilon)[:, None] * norm_gain[None, :]).astype(
        jnp.bfloat16
    )
    far_packet, stat_cols = held["packet"], held["stat_cols"]
    near_sum, near_top, near_den = held["near"]
    sum_shape = held["shape"]
    sum_cols = sum_shape[1] * sum_shape[2]
    far_sum = far_packet[:, :sum_cols].reshape(sum_shape)
    stat_parts = far_packet[:, sum_cols : sum_cols + 3 * stat_cols].astype(jnp.float32)
    far_stats = stat_parts[:, :stat_cols] + (
        stat_parts[:, stat_cols : 2 * stat_cols] + stat_parts[:, 2 * stat_cols :]
    )
    head_count = sum_shape[1]
    far_top, far_den = far_stats[:, :head_count], far_stats[:, head_count:]
    far_top = jnp.where(far_den > 0, far_top, jnp.float32(-1e30))
    top = jnp.maximum(near_top, far_top)
    near_scale = jnp.exp(near_top - top)
    far_scale = jnp.exp(far_top - top)
    denominator = near_den * near_scale + far_den * far_scale
    summed = near_sum * near_scale[:, :, None] + far_sum.astype(jnp.float32) * far_scale[:, :, None]
    attended = (summed / denominator[:, :, None]).astype(jnp.bfloat16).reshape(tok_rows, -1)
    return (normed, attended)


def solution(mesh):
    placed = (
        P("ctx", "tp"),
        P("ctx", "tp"),
        P("ctx", "tp"),
        P("ctx", "tp"),
        P("tp", None),
        P("tp"),
        P("ctx", "tp"),
        P("ctx", "tp"),
        P("ctx", "tp"),
        P(),
    )
    return jax.shard_map(
        block_body,
        mesh=mesh,
        in_specs=placed,
        out_specs=(P("ctx", "tp"), P("ctx", "tp")),
        check_vma=False,
    )
```

```python
import jax
import jax.numpy as jnp
from jax import lax
from jax.experimental import pallas as pl
from jax.experimental.pallas import tpu as pltpu
from jax.sharding import PartitionSpec as P

D = 8192
HEAD_DIM = 128


norm_epsilon = 1e-05


def shifted(value, axis, steps):
    count = lax.axis_size(axis)
    first, last = (max(0, -steps), min(count, count - steps))
    return lax.ppermute(value, axis, [(source, source + steps) for source in range(first, last)])


def document_begin(doc_lengths, positions):
    count = doc_lengths.shape[0]
    order = jnp.arange(count, dtype=jnp.int32)
    before = order[None, :] < order[:, None]
    starts = jnp.sum(jnp.where(before, doc_lengths[None, :], 0), axis=1)
    return jnp.max(jnp.where(starts[None, :] <= positions[:, None], starts[None, :], 0), axis=1)


def toeplitz_rows(reversed_ref, out_ref):
    rows = out_ref.shape[1]
    for group in range(out_ref.shape[0]):
        line = jnp.broadcast_to(reversed_ref[group : group + 1, :], (rows, reversed_ref.shape[1]))
        out_ref[group] = pltpu.roll(line, 0, 1, stride=1, stride_axis=0)


def build_toeplitz(filter_taps):
    groups, taps = filter_taps.shape
    span = 2 * taps
    reversed_taps = jnp.concatenate(
        [filter_taps[:, ::-1], jnp.zeros((groups, span - taps), jnp.float32)], axis=1
    )
    step = 8
    return pl.pallas_call(
        toeplitz_rows,
        grid=(groups // step,),
        in_specs=[pl.BlockSpec((step, span), lambda i: (i, 0))],
        out_specs=pl.BlockSpec((step, taps, span), lambda i: (i, 0, 0)),
        out_shape=jax.ShapeDtypeStruct((groups, taps, span), jnp.float32),
    )(reversed_taps)


def causal_filter(extended, filter_taps, reach_back, out_rows, between):
    groups, taps = filter_taps.shape
    channels = extended.shape[1]
    width = channels // groups
    span = 2 * taps
    lag_table = (
        jnp.arange(taps, dtype=jnp.int32)[:, None]
        + (taps - 1)
        - jnp.arange(span, dtype=jnp.int32)[None, :]
    )
    toeplitz = build_toeplitz(filter_taps)
    upper_part = toeplitz.astype(jnp.bfloat16)
    lower_part = (toeplitz - upper_part.astype(jnp.float32)).astype(jnp.bfloat16)
    zero_half = jnp.zeros((), jnp.bfloat16)
    numbers = (((0,), (2,)), ((1,), (0,)))
    extended = jnp.concatenate([extended, jnp.zeros((1, channels), extended.dtype)], axis=0)
    results = []
    for block_index in range(out_rows // taps):
        if block_index == 1:
            extended = between(results[0], extended)
        first = block_index * taps
        sources = extended[first : first + span].reshape(span, groups, width)
        limits = reach_back[first : first + taps]
        valid = (lag_table <= limits[:, None])[None]
        kernel_upper = jnp.where(valid, upper_part, zero_half)
        kernel_lower = jnp.where(valid, lower_part, zero_half)
        result = lax.dot_general(sources, kernel_upper, numbers, preferred_element_type=jnp.float32)
        result = result + lax.dot_general(
            sources, kernel_lower, numbers, preferred_element_type=jnp.float32
        )
        results.append(result.transpose(2, 0, 1).reshape(taps, channels))
    return jnp.concatenate(results, axis=0)


def tp_sum(value):
    count = lax.axis_size("tp")
    stride = 1
    while stride < count:
        value = value + lax.ppermute(value, "tp", [(i, i ^ stride) for i in range(count)])
        stride *= 2
    return value


def attend_block(queries, keys, values, visible, scale):
    head_count = queries.shape[1] // HEAD_DIM
    query_heads = queries.reshape(queries.shape[0], head_count, HEAD_DIM)
    key_heads = keys.reshape(keys.shape[0], head_count, HEAD_DIM)
    value_heads = values.reshape(values.shape[0], head_count, HEAD_DIM)
    scores = (
        jnp.einsum("qhd,khd->hqk", query_heads, key_heads, preferred_element_type=jnp.float32)
        * scale
    )
    scores = jnp.where(visible[None], scores, jnp.float32(-1e30))
    top = jnp.max(scores, axis=2, keepdims=True)
    expo = jnp.where(visible[None], jnp.exp(scores - top), jnp.float32(0.0))
    denominator = jnp.sum(expo, axis=2)
    summed = jnp.einsum(
        "hqk,khd->qhd", expo.astype(jnp.bfloat16), value_heads, preferred_element_type=jnp.float32
    )
    return summed, top[:, :, 0].T, denominator.T


def block_body(
    residual,
    hyena_gate,
    hyena_key,
    hyena_value,
    filter_taps,
    norm_gain,
    att_query,
    att_key,
    att_value,
    doc_lengths,
):
    tok_rows = residual.shape[0]
    taps = filter_taps.shape[1]
    shard_index = lax.axis_index("ctx")
    anchor = shard_index * tok_rows
    positions = anchor + jnp.arange(tok_rows, dtype=jnp.int32)
    doc_begin = document_begin(doc_lengths, positions)
    mixed_rows = (hyena_key.astype(jnp.float32) * hyena_value.astype(jnp.float32)).astype(
        jnp.bfloat16
    )
    rim_rows = shifted(mixed_rows[tok_rows - (taps - 1) :], "ctx", 1)
    key_pair = jnp.stack([att_key, att_value])
    previous = shifted(key_pair, "ctx", 1)
    later_query = shifted(att_query, "ctx", -2)
    key_rows = jnp.concatenate([previous[0], att_key], axis=0)
    value_rows = jnp.concatenate([previous[1], att_value], axis=0)
    window = key_rows.shape[0]
    key_pos = anchor - tok_rows + jnp.arange(window, dtype=jnp.int32)
    scale = jnp.float32(1.0 / HEAD_DIM**0.5)
    far_pos = positions + 2 * tok_rows
    far_begin = document_begin(doc_lengths, far_pos)
    far_visible = (key_pos[None, :] <= far_pos[:, None]) & (key_pos[None, :] >= far_begin[:, None])
    held = {}
    visible = (key_pos[None, :] <= positions[:, None]) & (key_pos[None, :] >= doc_begin[:, None])
    split = (att_query.shape[1] // HEAD_DIM // 2) * HEAD_DIM
    near_first = attend_block(
        att_query[:, :split], key_rows[:, :split], value_rows[:, :split], visible, scale
    )

    def far_part(first_rows, extended):
        first_rows, queries, held["near"] = lax.optimization_barrier(
            (first_rows, later_query, near_first)
        )
        far_sum, far_top, far_den = attend_block(queries, key_rows, value_rows, far_visible, scale)
        far_stats = jnp.concatenate([far_top, far_den], axis=1)
        stat_cols = far_stats.shape[1]
        stat_high = far_stats.astype(jnp.bfloat16)
        stat_rest = far_stats - stat_high.astype(jnp.float32)
        stat_mid = stat_rest.astype(jnp.bfloat16)
        stat_low = (stat_rest - stat_mid.astype(jnp.float32)).astype(jnp.bfloat16)
        stat_pad = jnp.zeros((tok_rows, 128 - 3 * stat_cols), jnp.bfloat16)
        far_packet = jnp.concatenate(
            [far_sum.astype(jnp.bfloat16).reshape(tok_rows, -1), stat_high, stat_mid, stat_low, stat_pad],
            axis=1,
        )
        far_packet, extended, held["late"] = lax.optimization_barrier(
            (far_packet, extended, (att_query[:, split:], key_rows[:, split:], value_rows[:, split:]))
        )
        held["packet"] = shifted(far_packet, "ctx", 2)
        held["shape"] = far_sum.shape
        held["stat_cols"] = stat_cols
        return extended

    extended = jnp.concatenate([rim_rows, mixed_rows], axis=0)
    filtered = causal_filter(extended, filter_taps, positions - doc_begin, tok_rows, far_part)
    hidden = residual.astype(jnp.float32) + hyena_gate.astype(jnp.float32) * filtered
    local_sum = jnp.sum(hidden * hidden, axis=1)
    mean_square = tp_sum(local_sum) / D
    normed = (hidden * lax.rsqrt(mean_square + norm_epsilon)[:, None] * norm_gain[None, :]).astype(
        jnp.bfloat16
    )
    far_packet, stat_cols = held["packet"], held["stat_cols"]
    late_query, late_key, late_value = held["late"]
    near_second = attend_block(late_query, late_key, late_value, visible, scale)
    near_sum = jnp.concatenate([held["near"][0], near_second[0]], axis=1)
    near_top = jnp.concatenate([held["near"][1], near_second[1]], axis=1)
    near_den = jnp.concatenate([held["near"][2], near_second[2]], axis=1)
    sum_shape = held["shape"]
    sum_cols = sum_shape[1] * sum_shape[2]
    far_sum = far_packet[:, :sum_cols].reshape(sum_shape)
    stat_parts = far_packet[:, sum_cols : sum_cols + 3 * stat_cols].astype(jnp.float32)
    far_stats = stat_parts[:, :stat_cols] + (
        stat_parts[:, stat_cols : 2 * stat_cols] + stat_parts[:, 2 * stat_cols :]
    )
    head_count = sum_shape[1]
    far_top, far_den = far_stats[:, :head_count], far_stats[:, head_count:]
    far_top = jnp.where(far_den > 0, far_top, jnp.float32(-1e30))
    top = jnp.maximum(near_top, far_top)
    near_scale = jnp.exp(near_top - top)
    far_scale = jnp.exp(far_top - top)
    denominator = near_den * near_scale + far_den * far_scale
    summed = near_sum * near_scale[:, :, None] + far_sum.astype(jnp.float32) * far_scale[:, :, None]
    attended = (summed / denominator[:, :, None]).astype(jnp.bfloat16).reshape(tok_rows, -1)
    return (normed, attended)


def solution(mesh):
    placed = (
        P("ctx", "tp"),
        P("ctx", "tp"),
        P("ctx", "tp"),
        P("ctx", "tp"),
        P("tp", None),
        P("tp"),
        P("ctx", "tp"),
        P("ctx", "tp"),
        P("ctx", "tp"),
        P(),
    )
    return jax.shard_map(
        block_body,
        mesh=mesh,
        in_specs=placed,
        out_specs=(P("ctx", "tp"), P("ctx", "tp")),
        check_vma=False,
    )
```

```python
import jax
import jax.numpy as jnp
from jax import lax
from jax.experimental import pallas as pl
from jax.experimental.pallas import tpu as pltpu
from jax.sharding import PartitionSpec as P

D = 8192
HEAD_DIM = 128


norm_epsilon = 1e-05


def shifted(value, axis, steps):
    count = lax.axis_size(axis)
    first, last = (max(0, -steps), min(count, count - steps))
    return lax.ppermute(value, axis, [(source, source + steps) for source in range(first, last)])


def document_begin(doc_lengths, positions):
    count = doc_lengths.shape[0]
    order = jnp.arange(count, dtype=jnp.int32)
    before = order[None, :] < order[:, None]
    starts = jnp.sum(jnp.where(before, doc_lengths[None, :], 0), axis=1)
    return jnp.max(jnp.where(starts[None, :] <= positions[:, None], starts[None, :], 0), axis=1)


def toeplitz_rows(reversed_ref, upper_ref, lower_ref):
    rows = upper_ref.shape[1]
    for group in range(upper_ref.shape[0]):
        line = jnp.broadcast_to(reversed_ref[group : group + 1, :], (rows, reversed_ref.shape[1]))
        rolled = pltpu.roll(line, 0, 1, stride=1, stride_axis=0)
        upper = rolled.astype(jnp.bfloat16)
        upper_ref[group] = upper
        lower_ref[group] = (rolled - upper.astype(jnp.float32)).astype(jnp.bfloat16)


def build_toeplitz(filter_taps):
    groups, taps = filter_taps.shape
    span = 2 * taps
    reversed_taps = jnp.concatenate(
        [filter_taps[:, ::-1], jnp.zeros((groups, span - taps), jnp.float32)], axis=1
    )
    step = 32
    part = jax.ShapeDtypeStruct((groups, taps, span), jnp.bfloat16)
    return pl.pallas_call(
        toeplitz_rows,
        grid=(groups // step,),
        in_specs=[pl.BlockSpec((step, span), lambda i: (i, 0))],
        out_specs=[pl.BlockSpec((step, taps, span), lambda i: (i, 0, 0))] * 2,
        out_shape=[part, part],
    )(reversed_taps)


def causal_filter(extended, filter_taps, reach_back, out_rows, between):
    groups, taps = filter_taps.shape
    channels = extended.shape[1]
    width = channels // groups
    span = 2 * taps
    lag_table = (
        jnp.arange(taps, dtype=jnp.int32)[:, None]
        + (taps - 1)
        - jnp.arange(span, dtype=jnp.int32)[None, :]
    )
    upper_part, lower_part = build_toeplitz(filter_taps)
    zero_half = jnp.zeros((), jnp.bfloat16)
    numbers = (((0,), (2,)), ((1,), (0,)))
    extended = jnp.concatenate([extended, jnp.zeros((1, channels), extended.dtype)], axis=0)
    results = []
    for block_index in range(out_rows // taps):
        if block_index == 1:
            extended = between(results[0], extended)
        first = block_index * taps
        sources = extended[first : first + span].reshape(span, groups, width)
        limits = reach_back[first : first + taps]
        valid = (lag_table <= limits[:, None])[None]
        kernel_upper = jnp.where(valid, upper_part, zero_half)
        kernel_lower = jnp.where(valid, lower_part, zero_half)
        result = lax.dot_general(sources, kernel_upper, numbers, preferred_element_type=jnp.float32)
        result = result + lax.dot_general(
            sources, kernel_lower, numbers, preferred_element_type=jnp.float32
        )
        results.append(result.transpose(2, 0, 1).reshape(taps, channels))
    return jnp.concatenate(results, axis=0)


def tp_sum(value):
    count = lax.axis_size("tp")
    stride = 1
    while stride < count:
        value = value + lax.ppermute(value, "tp", [(i, i ^ stride) for i in range(count)])
        stride *= 2
    return value


def attend_block(queries, keys, values, visible, scale):
    head_count = queries.shape[1] // HEAD_DIM
    query_heads = queries.reshape(queries.shape[0], head_count, HEAD_DIM)
    key_heads = keys.reshape(keys.shape[0], head_count, HEAD_DIM)
    value_heads = values.reshape(values.shape[0], head_count, HEAD_DIM)
    scores = (
        jnp.einsum("qhd,khd->hqk", query_heads, key_heads, preferred_element_type=jnp.float32)
        * scale
    )
    scores = jnp.where(visible[None], scores, jnp.float32(-1e30))
    top = jnp.max(scores, axis=2, keepdims=True)
    expo = jnp.where(visible[None], jnp.exp(scores - top), jnp.float32(0.0))
    denominator = jnp.sum(expo, axis=2)
    summed = jnp.einsum(
        "hqk,khd->qhd", expo.astype(jnp.bfloat16), value_heads, preferred_element_type=jnp.float32
    )
    return summed, top[:, :, 0].T, denominator.T


def block_body(
    residual,
    hyena_gate,
    hyena_key,
    hyena_value,
    filter_taps,
    norm_gain,
    att_query,
    att_key,
    att_value,
    doc_lengths,
):
    tok_rows = residual.shape[0]
    taps = filter_taps.shape[1]
    shard_index = lax.axis_index("ctx")
    anchor = shard_index * tok_rows
    positions = anchor + jnp.arange(tok_rows, dtype=jnp.int32)
    doc_begin = document_begin(doc_lengths, positions)
    mixed_rows = (hyena_key.astype(jnp.float32) * hyena_value.astype(jnp.float32)).astype(
        jnp.bfloat16
    )
    rim_rows = shifted(mixed_rows[tok_rows - (taps - 1) :], "ctx", 1)
    key_pair = jnp.stack([att_key, att_value])
    previous = shifted(key_pair, "ctx", 1)
    later_query = shifted(att_query, "ctx", -2)
    key_rows = jnp.concatenate([previous[0], att_key], axis=0)
    value_rows = jnp.concatenate([previous[1], att_value], axis=0)
    window = key_rows.shape[0]
    key_pos = anchor - tok_rows + jnp.arange(window, dtype=jnp.int32)
    scale = jnp.float32(1.0 / HEAD_DIM**0.5)
    far_pos = positions + 2 * tok_rows
    far_begin = document_begin(doc_lengths, far_pos)
    far_visible = (key_pos[None, :] <= far_pos[:, None]) & (key_pos[None, :] >= far_begin[:, None])
    held = {}
    visible = (key_pos[None, :] <= positions[:, None]) & (key_pos[None, :] >= doc_begin[:, None])
    near_sum, near_top, near_den = attend_block(att_query, key_rows, value_rows, visible, scale)

    def far_part(first_rows, extended):
        first_rows, queries, held["near"] = lax.optimization_barrier(
            (first_rows, later_query, (near_sum, near_top, near_den))
        )
        far_sum, far_top, far_den = attend_block(queries, key_rows, value_rows, far_visible, scale)
        far_stats = jnp.concatenate([far_top, far_den], axis=1)
        stat_cols = far_stats.shape[1]
        stat_high = far_stats.astype(jnp.bfloat16)
        stat_rest = far_stats - stat_high.astype(jnp.float32)
        stat_mid = stat_rest.astype(jnp.bfloat16)
        stat_low = (stat_rest - stat_mid.astype(jnp.float32)).astype(jnp.bfloat16)
        stat_pad = jnp.zeros((tok_rows, 128 - 3 * stat_cols), jnp.bfloat16)
        far_packet = jnp.concatenate(
            [far_sum.astype(jnp.bfloat16).reshape(tok_rows, -1), stat_high, stat_mid, stat_low, stat_pad],
            axis=1,
        )
        far_packet, extended = lax.optimization_barrier((far_packet, extended))
        held["packet"] = shifted(far_packet, "ctx", 2)
        held["shape"] = far_sum.shape
        held["stat_cols"] = stat_cols
        return extended

    extended = jnp.concatenate([rim_rows, mixed_rows], axis=0)
    filtered = causal_filter(extended, filter_taps, positions - doc_begin, tok_rows, far_part)
    hidden = residual.astype(jnp.float32) + hyena_gate.astype(jnp.float32) * filtered
    local_sum = jnp.sum(hidden * hidden, axis=1)
    mean_square = tp_sum(local_sum) / D
    normed = (hidden * lax.rsqrt(mean_square + norm_epsilon)[:, None] * norm_gain[None, :]).astype(
        jnp.bfloat16
    )
    far_packet, stat_cols = held["packet"], held["stat_cols"]
    near_sum, near_top, near_den = held["near"]
    sum_shape = held["shape"]
    sum_cols = sum_shape[1] * sum_shape[2]
    far_sum = far_packet[:, :sum_cols].reshape(sum_shape)
    stat_parts = far_packet[:, sum_cols : sum_cols + 3 * stat_cols].astype(jnp.float32)
    far_stats = stat_parts[:, :stat_cols] + (
        stat_parts[:, stat_cols : 2 * stat_cols] + stat_parts[:, 2 * stat_cols :]
    )
    head_count = sum_shape[1]
    far_top, far_den = far_stats[:, :head_count], far_stats[:, head_count:]
    far_top = jnp.where(far_den > 0, far_top, jnp.float32(-1e30))
    top = jnp.maximum(near_top, far_top)
    near_scale = jnp.exp(near_top - top)
    far_scale = jnp.exp(far_top - top)
    denominator = near_den * near_scale + far_den * far_scale
    summed = near_sum * near_scale[:, :, None] + far_sum.astype(jnp.float32) * far_scale[:, :, None]
    attended = (summed / denominator[:, :, None]).astype(jnp.bfloat16).reshape(tok_rows, -1)
    return (normed, attended)


def solution(mesh):
    placed = (
        P("ctx", "tp"),
        P("ctx", "tp"),
        P("ctx", "tp"),
        P("ctx", "tp"),
        P("tp", None),
        P("tp"),
        P("ctx", "tp"),
        P("ctx", "tp"),
        P("ctx", "tp"),
        P(),
    )
    return jax.shard_map(
        block_body,
        mesh=mesh,
        in_specs=placed,
        out_specs=(P("ctx", "tp"), P("ctx", "tp")),
        check_vma=False,
    )
```
